32 devices in a mesh: dp: 2 (over y), expert: 16 (over z, x, core).
Axes of the slice: x: 2, y: 2, z: 4, core: 2. Of those that a mesh axis runs over, the one named last changes fastest.
Arguments:
- attention: bfloat16 [16, 2, 16, 1024], P('expert', 'dp'), may hold values from -6 to 6
- residual: bfloat16 [16, 2, 16, 2048], P('expert', 'dp')
- out_proj: bfloat16 [1024, 2048], P(None, 'dp'), may hold values from -0.1875 to 0.1875
- gain_in: float32 [2048], replicated, may hold values from 0.5 to 1.5
- router: bfloat16 [2048, 16], P(None, 'dp')
- expert_ids: int32 [16, 2, 16, 6], P('expert'), may hold values from 0 to 15, all different within a row; in each aligned block of 16 rows (0 to 15, 16 to 31, ..., all dimensions but the last counted through in order) at most 12 rows name the same one
- live_rows: int32 [2, 16], P(None, 'expert'), may hold values from 1 to 16, 224 in all within a row
- expert_gate: bfloat16 [16, 1408, 2048], P('expert', 'dp'), may hold values from -0.25 to 0.25
- expert_up: bfloat16 [16, 1408, 2048], P('expert', 'dp'), may hold values from -0.25 to 0.25
- expert_down: bfloat16 [16, 1408, 2048], P('expert', None, 'dp'), may hold values from -0.15625 to 0.15625
- shared_gate: bfloat16 [1408, 2048], P('dp'), may hold values from -0.125 to 0.125
- shared_up: bfloat16 [1408, 2048], P('dp'), may hold values from -0.125 to 0.125
- shared_down: bfloat16 [1408, 2048], P(None, 'dp'), may hold values from -0.15625 to 0.15625
- gain_out: float32 [2048], replicated, may hold values from 0.5 to 1.5
Outputs:
- stream: bfloat16 [16, 2, 16, 2048], P('expert', 'dp')
- normed: bfloat16 [16, 2, 16, 2048], P('expert', 'dp')
The draws below stay inside these ranges and needn't reach their ends.
Inputs may be any that keep to these rules, and one draw needn't show every extreme that they name: `expert_ids`: each row names 6 different experts; the 16 rows of one block [o, g] name one expert at most 12 times, a bound that some block reaches. The live rows of a device are its first live_rows[g, o]; the 16 counts of each g sum to 224, and one of them is 16.
All inputs are finite; a program needn't handle non-finite values.
Results may differ from the reference program's by a relative error of at most 0.0095.
Values may be sent and summed in bfloat16 or wider, within the bound.
No kernel may reach another device: no remote copies, remote signals or barrier semaphores. Data moves between devices by JAX's collectives and lax.ppermute only.
A program may use at most 128 MiB of HBM per device.

```python
import math
import jax
import jax.numpy as jnp
import numpy as np
from jax import lax

D = 2048
FF_E = 1408
TOPK = 6
HW = 1024
SH_FF = 1408
ROWS = 16
GROUPS = 2
OWNERS = 16
EXPERTS = 16
CAP = 12


def draw_residual(key, part):
    key_base = jax.random.fold_in(key, 11)
    key_rows = jax.random.fold_in(key, 12)
    key_cols = jax.random.fold_in(key, 13)
    shape = (OWNERS, GROUPS, ROWS, D)
    base_draw = jnp.clip(jax.random.normal(key_base, shape, jnp.float32), -6.0, 6.0)
    row_scale = jnp.exp(jax.random.uniform(key_rows, (OWNERS, GROUPS, ROWS, 1), jnp.float32, 0.0, math.log(10.0)))
    col_scale = jnp.exp(jax.random.uniform(key_cols, (D,), jnp.float32, 0.0, math.log(10.0)))
    return (base_draw * row_scale * col_scale * 0.02).astype(jnp.bfloat16)


def draw_router(key, part):
    key_base = jax.random.fold_in(key, 21)
    key_cols = jax.random.fold_in(key, 22)
    base_draw = jnp.clip(jax.random.normal(key_base, (D, EXPERTS), jnp.float32), -6.0, 6.0) * D ** (-0.5)
    drawn_scale = jax.random.uniform(key_cols, (EXPERTS,), jnp.float32, 1.0, 1.2)
    col_scale = drawn_scale
    return (base_draw * col_scale).astype(jnp.bfloat16)


def level_of(stream_key, extent, cuts, smallest, top_value):
    def one(dim, blocks):
        steps = jax.random.uniform(jax.random.fold_in(jax.random.fold_in(stream_key, 6), dim), (blocks,), jnp.float32, smallest / len(cuts), top_value / len(cuts))
        return jnp.repeat(jnp.exp(steps), extent[dim] // blocks).reshape((-1,) + (1,) * (len(extent) - dim - 1))

    level = one(*cuts[0])
    for cut in cuts[1:]:
        level = level * one(*cut)
    return level


def length_profile(count, total, most, slope):
    loads = [(1 << 20) // math.isqrt(rank ** slope) + 1 for rank in range(2, count + 1)]
    rest, holding = total - most - (count - 1), [1] * (count - 1)
    while rest > 0:
        free = [i for i in range(count - 1) if holding[i] < most]
        whole, remaining = sum([loads[i] for i in free]), rest
        for i in free:
            extra = min(most - holding[i], max(1, remaining * loads[i] // whole), rest)
            holding[i] = holding[i] + extra
            rest = rest - extra
    return np.array([most] + holding)


def ragged(own_key, number_of, total, reach, skew):
    if number_of == 2:
        one = jax.random.randint(own_key, (), max(1, total - reach), min(reach, total - 1) + 1)
        return jnp.stack([one, total - one])
    tallies = jnp.asarray(length_profile(number_of, total, reach, skew), jnp.int32)
    pairs = (number_of - 1) // 2
    giver, taker = tallies[1:1 + 2 * pairs:2], tallies[2:2 + 2 * pairs:2]
    slack = jnp.minimum(giver - 1, reach - taker)
    passed = jax.random.randint(jax.random.fold_in(own_key, 1), (pairs,), 0, 1 << 20) % (slack + 1)
    tallies = tallies.at[1:1 + 2 * pairs:2].set(giver - passed).at[2:2 + 2 * pairs:2].set(taker + passed)
    return tallies[jax.random.permutation(jax.random.fold_in(own_key, 2), number_of)]


def deal_out(own_key, own, number, rows, number_of, top, limit, slope):
    sequence = jax.random.permutation(own_key, number_of)
    packed, common = load_shares(number_of, rows * top, limit, slope, True), load_shares(number_of, rows * top, limit, slope, False)
    places = jnp.arange(number_of)

    def named(tallies, offset_by):
        used = int((tallies > 0).sum())
        fixed = max(1, used // 4)
        passed = fixed + (places - fixed + offset_by * (used - fixed)) % max(1, number_of - fixed)
        return jnp.zeros((number_of,), jnp.int32).at[sequence[jnp.where(places < fixed, places, passed)]].set(jnp.asarray(tallies, jnp.int32))

    tallies = jnp.where(number % 4 == 0, named(packed, number // 4), named(common, number - number // 4 - 1))
    mixed = jax.random.permutation(jax.random.fold_in(own, 3), number_of)
    donor, taker = mixed[0:number_of // 2 * 2:2], mixed[1:number_of // 2 * 2:2]
    margin = jnp.minimum(tallies[donor] - 1, limit - tallies[taker]) // 2
    margin = jnp.where((donor == sequence[0]) | (taker == sequence[0]) | (tallies[taker] == 0), 0, jnp.maximum(margin, 0))
    passed = jax.random.randint(jax.random.fold_in(own, 4), (number_of // 2,), 0, 1 << 20) % (margin + 1)
    tallies = tallies.at[donor].add(-passed).at[taker].add(passed)
    items = jnp.searchsorted(jnp.cumsum(tallies), jnp.arange(rows * top), side="right").astype(jnp.int32)
    table = items.reshape(top, rows).T
    table = table[jax.random.permutation(jax.random.fold_in(own, 1), rows)]
    offset_by = jax.random.randint(jax.random.fold_in(own, 2), (rows, 1), 0, top)
    return jnp.take_along_axis(table, (jnp.arange(top)[None, :] + offset_by) % top, axis=1)


def load_shares(count, total, limit, skew, full):
    weights = [(1 << 20) // math.isqrt(grade ** skew) + 1 for grade in range(1, count + 1)]
    largest = limit if full else min(limit, max(-(-total // count), total * weights[0] // sum(weights)))
    least = 1 if total - largest >= count - 1 else 0
    counts, rest = [largest] + [least] * (count - 1), total - largest - least * (count - 1)
    while rest > 0:
        movable = [i for i in range(1, count) if counts[i] < largest] or [i for i in range(1, count) if counts[i] < limit]
        whole, left = sum([weights[i] for i in movable]), rest
        for i in movable:
            addition = min(limit - counts[i], max(1, left * weights[i] // whole), rest)
            counts[i] = counts[i] + addition
            rest = rest - addition
    return np.array(counts)


def gaussian(rng, dims, width, limit, pieces=(), kind=jnp.bfloat16):
    array = width * jax.random.normal(rng, dims, jnp.float32)
    if pieces:
        array = array * level_of(rng, dims, pieces, -0.22, 0.18)
    return jnp.clip(array, -limit, limit).astype(kind)


def setup_inputs(seed: int = 0) -> dict:
    arg_keys = jax.random.split(jax.random.key(seed), 15)
    attention = gaussian(arg_keys[0], (OWNERS, GROUPS, ROWS, HW), 1.0, 6.0, ((0, 16), (1, 2)))
    residual = draw_residual(jax.random.fold_in(arg_keys[14], 71), 0)
    out_proj = gaussian(arg_keys[2], (HW, D), HW ** -0.5, 0.1875, ((1, 2),))
    gain_in = jnp.clip(1.0 + 0.1 * jax.random.normal(arg_keys[3], (D,), jnp.float32), 0.5, 1.5)
    router = draw_router(jax.random.fold_in(arg_keys[14], 71), 0)
    expert_ids_keys = jax.random.split(jax.random.fold_in(arg_keys[5], 1), OWNERS * GROUPS * ROWS // ROWS)
    expert_ids_turns = jax.random.permutation(jax.random.fold_in(arg_keys[5], 3), OWNERS * GROUPS * ROWS // ROWS)
    expert_ids = jax.vmap(lambda own, number: deal_out(jax.random.fold_in(arg_keys[5], 2), own, number, ROWS, EXPERTS, TOPK, CAP, 2))(expert_ids_keys, expert_ids_turns).reshape((OWNERS, GROUPS, ROWS, TOPK))
    live_rows = jax.vmap(lambda own: ragged(own, OWNERS, OWNERS * ROWS * 7 // 8, ROWS, 1))(jax.random.split(arg_keys[6], GROUPS)).reshape((GROUPS, OWNERS)).astype(jnp.int32)
    expert_gate = gaussian(arg_keys[7], (EXPERTS, FF_E, D), (D // 4) ** -0.5, 0.25, ((0, 16), (1, 2)))
    expert_up = gaussian(arg_keys[8], (EXPERTS, FF_E, D), (D // 4) ** -0.5, 0.25, ((0, 16), (1, 2)))
    expert_down = gaussian(arg_keys[9], (EXPERTS, FF_E, D), FF_E ** -0.5, 0.15625, ((0, 16), (2, 2)))
    shared_gate = gaussian(arg_keys[10], (SH_FF, D), D ** -0.5, 0.125, ((0, 2),))
    shared_up = gaussian(arg_keys[11], (SH_FF, D), D ** -0.5, 0.125, ((0, 2),))
    shared_down = gaussian(arg_keys[12], (SH_FF, D), SH_FF ** -0.5, 0.15625, ((1, 2),))
    gain_out = jnp.clip(1.0 + 0.1 * jax.random.normal(arg_keys[13], (D,), jnp.float32), 0.5, 1.5)
    return dict(attention=attention, residual=residual, out_proj=out_proj, gain_in=gain_in, router=router, expert_ids=expert_ids, live_rows=live_rows, expert_gate=expert_gate, expert_up=expert_up, expert_down=expert_down, shared_gate=shared_gate, shared_up=shared_up, shared_down=shared_down, gain_out=gain_out)


def rms_scale(features, scale_gain):
    return features * lax.rsqrt(lax.optimization_barrier(jnp.mean(features * features, axis=-1, keepdims=True)) + 1e-06) * scale_gain

def by_rows(left, weight_rows):
    return lax.dot_general(left, weight_rows, (((1,), (1,)), ((), ())), preferred_element_type=jnp.float32)

def reference(attention, residual, out_proj, gain_in, router, expert_ids, live_rows, expert_gate, expert_up, expert_down, shared_gate, shared_up, shared_down, gain_out):
    blocks = OWNERS * GROUPS
    row_total = blocks * ROWS
    flattened = attention.reshape(row_total, HW)
    projected = jnp.dot(flattened, out_proj, preferred_element_type=jnp.float32).astype(jnp.bfloat16)
    stream_in = residual.reshape(row_total, D).astype(jnp.float32) + projected.astype(jnp.float32)
    normal_rows = rms_scale(stream_in, gain_in).astype(jnp.bfloat16)
    logits = jnp.dot(normal_rows, router, preferred_element_type=jnp.float32)
    flat_experts = expert_ids.reshape(row_total, TOPK).astype(jnp.int32)
    picked = jnp.take_along_axis(logits, flat_experts, axis=1)
    rounded = lax.optimization_barrier(jax.nn.softmax(picked, axis=1).astype(jnp.bfloat16))
    weights = rounded.astype(jnp.float32)
    row_live = (jnp.arange(ROWS, dtype=jnp.int32)[None, :] < jnp.transpose(live_rows).reshape(blocks, 1).astype(jnp.int32)).reshape(row_total)
    slot_live = jnp.broadcast_to(row_live[:, None], (row_total, TOPK))
    block_experts = flat_experts.reshape(blocks, ROWS * TOPK)
    block_live = slot_live.reshape(blocks, ROWS * TOPK)
    onehot = ((block_experts[:, :, None] == jnp.arange(EXPERTS, dtype=jnp.int32)) & block_live[:, :, None]).astype(jnp.int32)
    before = jnp.cumsum(onehot, axis=1) - onehot
    position = lax.optimization_barrier(jnp.sum(before * onehot, axis=2))
    slot_index = (jnp.arange(blocks, dtype=jnp.int32)[:, None] * CAP + position).reshape(-1).astype(jnp.int32)
    slot_expert = block_experts.reshape(-1)
    slot_ok = block_live.reshape(-1)
    slot_weight = weights.reshape(-1)
    slot_count = blocks * CAP
    entries = jnp.arange(row_total * TOPK, dtype=jnp.int32)

    def one_expert(routed, members):
        gate_weight, up_weight, down_weight, expert_index = members
        target = jnp.where(slot_ok & (slot_expert == expert_index), slot_index, slot_count).astype(jnp.int32)
        source = jnp.full((slot_count,), -1, jnp.int32).at[target].set(entries, mode='drop')
        is_valid = source >= 0
        safe_source = jnp.maximum(source, 0).astype(jnp.int32)
        row_index = (safe_source // TOPK).astype(jnp.int32)
        chosen = jnp.take(normal_rows, row_index, axis=0)
        gate_value = by_rows(chosen, gate_weight)
        up_value = by_rows(chosen, up_weight)
        hidden = (jax.nn.silu(gate_value) * up_value).astype(jnp.bfloat16)
        output = jnp.dot(hidden, down_weight, preferred_element_type=jnp.float32).astype(jnp.bfloat16).astype(jnp.float32)
        slot_scale = jnp.where(is_valid, jnp.take(slot_weight, safe_source), jnp.zeros((slot_count,), jnp.float32))
        return (routed.at[row_index].add(output * slot_scale[:, None]), None)
    routed, leftover = lax.scan(one_expert, jnp.zeros((row_total, D), jnp.float32), (expert_gate, expert_up, expert_down, jnp.arange(EXPERTS, dtype=jnp.int32)))
    shared_gate_value = by_rows(normal_rows, shared_gate)
    shared_up_value = by_rows(normal_rows, shared_up)
    shared_hidden = (jax.nn.silu(shared_gate_value) * shared_up_value).astype(jnp.bfloat16)
    shared = jnp.dot(shared_hidden, shared_down, preferred_element_type=jnp.float32)
    stream_sum = stream_in + jnp.where(row_live[:, None], routed + shared, jnp.zeros((row_total, D), jnp.float32))
    stream = stream_sum.astype(jnp.bfloat16).reshape(OWNERS, GROUPS, ROWS, D)
    normed = rms_scale(stream_sum, gain_out).astype(jnp.bfloat16).reshape(OWNERS, GROUPS, ROWS, D)
    return (stream, normed)
```

```python
import jax
import jax.numpy as jnp
from jax import lax
from jax.sharding import PartitionSpec as P


def rms_scale(features, scale_gain):
    return (
        features
        * lax.rsqrt(jnp.mean(features * features, axis=-1, keepdims=True) + 1e-06)
        * scale_gain
    )


def by_rows(left, weight_rows):
    return lax.dot_general(
        left, weight_rows, (((1,), (1,)), ((), ())), preferred_element_type=jnp.float32
    )


def gather_axis(x, name, axis):
    n = lax.axis_size(name)
    if n == 1:
        return x
    me = lax.axis_index(name)
    pieces = [x]
    for shift in range(1, n):
        pieces.append(lax.ppermute(x, name, [(j, (j + shift) % n) for j in range(n)]))
    if n == 2:
        first = jnp.where(me == 0, pieces[0], pieces[1])
        second = jnp.where(me == 0, pieces[1], pieces[0])
        ordered = [first, second]
        return jnp.concatenate(ordered, axis=axis)
    stacked = jnp.stack(pieces, 0)
    order = (me - jnp.arange(n)) % n
    ordered = jnp.take(stacked, order, axis=0)
    ordered = jnp.moveaxis(ordered, 0, axis)
    shape = list(x.shape)
    shape[axis] = shape[axis] * n
    return ordered.reshape(shape)


def shards(
    attention,
    residual,
    out_proj,
    gain_in,
    router,
    expert_ids,
    live_rows,
    expert_gate,
    expert_up,
    expert_down,
    shared_gate,
    shared_up,
    shared_down,
    gain_out,
):
    groups = lax.axis_size("dp")
    experts = lax.axis_size("expert")
    row_count = attention.shape[2]
    feature_width = residual.shape[3]
    top_count = expert_ids.shape[3]
    capacity = max(2, (2 * row_count * top_count + experts - 1) // experts)
    gate_local = expert_gate[0]
    up_local = expert_up[0]
    down_local = expert_down[0]
    column_width = down_local.shape[1]
    rows_all = groups * row_count

    pieces = gather_axis(attention, "dp", 1)
    flattened = pieces.reshape(-1, pieces.shape[-1])
    product = jnp.dot(flattened, out_proj, preferred_element_type=jnp.float32).astype(jnp.bfloat16)
    columns = product.reshape(pieces.shape[:-1] + (out_proj.shape[1],))
    projected = lax.all_to_all(columns, "dp", split_axis=1, concat_axis=3, tiled=True)[0, 0]
    stream_in = residual[0, 0].astype(jnp.float32) + projected.astype(jnp.float32)
    normal_rows = rms_scale(stream_in, gain_in).astype(jnp.bfloat16)
    column = gather_axis(normal_rows, "dp", 0)
    logit_part = jnp.dot(column, router, preferred_element_type=jnp.float32)
    logits = gather_axis(logit_part, "dp", 1)
    flat_experts = expert_ids[0].reshape(rows_all, top_count)
    picked = jnp.take_along_axis(logits, flat_experts, axis=1)
    probabilities = jax.nn.softmax(picked, axis=1)
    row_live = (jnp.arange(row_count, dtype=jnp.int32)[None, :] < live_rows[:, 0][:, None]).reshape(
        rows_all
    )
    slot_live = jnp.broadcast_to(row_live[:, None], (rows_all, top_count))
    weights = probabilities.astype(jnp.bfloat16) * slot_live.astype(jnp.bfloat16)
    block_experts = flat_experts.reshape(groups, row_count * top_count)
    block_live = slot_live.reshape(groups, row_count * top_count)
    onehot = (
        (block_experts[:, :, None] == jnp.arange(experts, dtype=jnp.int32)) & block_live[:, :, None]
    ).astype(jnp.int32)
    before = jnp.cumsum(onehot, axis=1) - onehot
    position = jnp.sum(before * onehot, axis=2)
    slot_total = experts * groups * capacity
    offsets = jnp.arange(groups, dtype=jnp.int32)[:, None] * capacity
    target = jnp.where(
        block_live, block_experts * (groups * capacity) + offsets + position, slot_total
    ).reshape(rows_all, top_count)
    slot_hit = target[:, :, None] == jnp.arange(slot_total, dtype=jnp.int32)[None, None, :]
    fill = jnp.any(slot_hit, axis=1).astype(jnp.bfloat16)
    outgoing = lax.dot_general(
        fill, column, (((0,), (0,)), ((), ())), preferred_element_type=jnp.float32
    ).astype(jnp.bfloat16).reshape(experts, groups * capacity, feature_width)
    slot_rows = lax.all_to_all(outgoing, "expert", split_axis=0, concat_axis=0, tiled=True)
    flattened = slot_rows.reshape(-1, slot_rows.shape[-1])
    gate_value = by_rows(flattened, gate_local)
    up_value = by_rows(flattened, up_local)
    hidden = (jax.nn.silu(gate_value) * up_value).astype(jnp.bfloat16)
    shared_gate_value = by_rows(column, shared_gate)
    shared_up_value = by_rows(column, shared_up)
    shared_hidden = (jax.nn.silu(shared_gate_value) * shared_up_value).astype(jnp.bfloat16)
    routed_piece = gather_axis(hidden, "dp", 1)
    shared_piece = gather_axis(shared_hidden, "dp", 1)
    routed_total = jnp.dot(routed_piece, down_local, preferred_element_type=jnp.float32)
    shared = jnp.dot(shared_piece, shared_down, preferred_element_type=jnp.float32)
    expert_out = routed_total.astype(jnp.bfloat16).reshape(experts, groups * capacity, column_width)
    returned = lax.all_to_all(
        expert_out, "expert", split_axis=0, concat_axis=0, tiled=True
    ).reshape(slot_total, column_width)
    combine = jnp.sum(
        jnp.where(slot_hit, weights[:, :, None], jnp.zeros((), jnp.bfloat16)), axis=1
    ).astype(jnp.bfloat16)
    routed = jnp.dot(combine, returned, preferred_element_type=jnp.float32)
    combined = jnp.where(row_live[:, None], routed + shared, 0.0).reshape(
        groups, row_count, column_width
    )
    summed = lax.all_to_all(combined, "dp", split_axis=0, concat_axis=2, tiled=True)[0]
    stream_sum = stream_in + summed
    stream = stream_sum.astype(jnp.bfloat16)[None, None]
    normed = rms_scale(stream_sum, gain_out).astype(jnp.bfloat16)[None, None]
    return (stream, normed)


def solution(mesh):
    placed = (
        P("expert", "dp", None, None),
        P("expert", "dp", None, None),
        P(None, "dp"),
        P(),
        P(None, "dp"),
        P("expert", None, None, None),
        P(None, "expert"),
        P("expert", "dp", None),
        P("expert", "dp", None),
        P("expert", None, "dp"),
        P("dp", None),
        P("dp", None),
        P(None, "dp"),
        P(),
    )
    return jax.shard_map(
        shards,
        mesh=mesh,
        in_specs=placed,
        out_specs=(P("expert", "dp", None, None), P("expert", "dp", None, None)),
        check_vma=False,
    )
```

```python
import jax
import jax.numpy as jnp
from jax import lax
from jax.sharding import PartitionSpec as P


def rms_scale(features, scale_gain):
    return (
        features
        * lax.rsqrt(jnp.mean(features * features, axis=-1, keepdims=True) + 1e-06)
        * scale_gain
    )


def by_rows(left, weight_rows):
    return lax.dot_general(
        left, weight_rows, (((1,), (1,)), ((), ())), preferred_element_type=jnp.float32
    )


def fill_slots(features, targets, slot_total, top_count):
    entries = jnp.arange(targets.shape[0], dtype=jnp.int32)
    source = jnp.full((slot_total,), -1, jnp.int32).at[targets].set(entries, mode="drop")
    chosen = jnp.take(features, jnp.maximum(source, 0) // top_count, axis=0)
    return jnp.where((source >= 0)[:, None], chosen, jnp.zeros_like(chosen))


def shards_general(
    attention,
    residual,
    out_proj,
    gain_in,
    router,
    expert_ids,
    live_rows,
    expert_gate,
    expert_up,
    expert_down,
    shared_gate,
    shared_up,
    shared_down,
    gain_out,
):
    groups = lax.axis_size("dp")
    experts = lax.axis_size("expert")
    row_count = attention.shape[2]
    feature_width = residual.shape[3]
    top_count = expert_ids.shape[3]
    capacity = max(2, (2 * row_count * top_count + experts - 1) // experts)
    gate_local = expert_gate[0]
    up_local = expert_up[0]
    down_local = expert_down[0]
    column_width = down_local.shape[1]
    pieces = lax.all_gather(attention, "dp", axis=1, tiled=True)
    flattened = pieces.reshape(-1, pieces.shape[-1])
    product = jnp.dot(flattened, out_proj, preferred_element_type=jnp.float32).astype(jnp.bfloat16)
    columns = product.reshape(pieces.shape[:-1] + (out_proj.shape[1],))
    projected = lax.all_to_all(columns, "dp", split_axis=1, concat_axis=3, tiled=True)[0, 0]
    stream_in = residual[0, 0].astype(jnp.float32) + projected.astype(jnp.float32)
    normal_rows = rms_scale(stream_in, gain_in).astype(jnp.bfloat16)
    column = lax.all_gather(normal_rows[None], "dp", axis=0, tiled=True).reshape(
        groups * row_count, feature_width
    )
    logit_part = jnp.dot(column, router, preferred_element_type=jnp.float32)
    logits = lax.all_gather(logit_part, "dp", axis=1, tiled=True)
    flat_experts = expert_ids[0].reshape(groups * row_count, top_count)
    picked = jnp.take_along_axis(logits, flat_experts, axis=1)
    probabilities = jax.nn.softmax(picked, axis=1)
    row_live = (jnp.arange(row_count, dtype=jnp.int32)[None, :] < live_rows[:, 0][:, None]).reshape(
        groups * row_count
    )
    slot_live = jnp.broadcast_to(row_live[:, None], (groups * row_count, top_count))
    weights = probabilities.astype(jnp.bfloat16) * slot_live.astype(jnp.bfloat16)
    block_experts = flat_experts.reshape(groups, row_count * top_count)
    block_live = slot_live.reshape(groups, row_count * top_count)
    onehot = (
        (block_experts[:, :, None] == jnp.arange(experts, dtype=jnp.int32)) & block_live[:, :, None]
    ).astype(jnp.int32)
    before = jnp.cumsum(onehot, axis=1) - onehot
    position = jnp.sum(before * onehot, axis=2)
    slot_total = experts * groups * capacity
    offsets = jnp.arange(groups, dtype=jnp.int32)[:, None] * capacity
    target = jnp.where(
        block_live, block_experts * (groups * capacity) + offsets + position, slot_total
    ).reshape(-1)
    outgoing = fill_slots(column, target, slot_total, top_count).reshape(
        experts, groups * capacity, feature_width
    )
    slot_rows = lax.all_to_all(outgoing, "expert", split_axis=0, concat_axis=0, tiled=True)
    flattened = slot_rows.reshape(-1, slot_rows.shape[-1])
    gate_value = by_rows(flattened, gate_local)
    up_value = by_rows(flattened, up_local)
    hidden = (jax.nn.silu(gate_value) * up_value).astype(jnp.bfloat16)
    routed_hidden = hidden.reshape(slot_rows.shape[:-1] + (gate_local.shape[0],))
    shared_gate_value = by_rows(column, shared_gate)
    shared_up_value = by_rows(column, shared_up)
    shared_hidden = (jax.nn.silu(shared_gate_value) * shared_up_value).astype(jnp.bfloat16)[None]
    routed_piece = lax.all_gather(routed_hidden, "dp", axis=2, tiled=True)
    shared_piece = lax.all_gather(shared_hidden, "dp", axis=2, tiled=True)
    count = routed_piece.shape[2]
    routed_total = jnp.dot(
        routed_piece.reshape(-1, count), down_local, preferred_element_type=jnp.float32
    )
    shared_total = jnp.dot(
        shared_piece.reshape(-1, shared_piece.shape[2]),
        shared_down,
        preferred_element_type=jnp.float32,
    )
    routed_total, shared = (routed_total, shared_total)
    expert_out = routed_total.astype(jnp.bfloat16).reshape(experts, groups * capacity, column_width)
    returned = lax.all_to_all(
        expert_out, "expert", split_axis=0, concat_axis=0, tiled=True
    ).reshape(slot_total, column_width)
    gathered = jnp.take(returned, jnp.minimum(target, slot_total - 1), axis=0).reshape(
        groups * row_count, top_count, column_width
    )
    routed = jnp.einsum("nk,nkd->nd", weights, gathered, preferred_element_type=jnp.float32)
    combined = jnp.where(row_live[:, None], routed + shared, 0.0).reshape(
        groups, row_count, column_width
    )
    summed = lax.all_to_all(combined, "dp", split_axis=0, concat_axis=2, tiled=True)[0]
    stream_sum = stream_in + summed
    stream = stream_sum.astype(jnp.bfloat16)[None, None]
    normed = rms_scale(stream_sum, gain_out).astype(jnp.bfloat16)[None, None]
    return (stream, normed)


def swap_pair(x):
    return lax.ppermute(x, "dp", [(0, 1), (1, 0)])


def halves_swapped(x):
    half = x.shape[0] // 2
    return jnp.concatenate([x[half:], x[:half]], axis=0)


def in_axis_order(first, mine, peer, axis):
    return jnp.where(
        first, jnp.concatenate([mine, peer], axis=axis), jnp.concatenate([peer, mine], axis=axis)
    )


def shards_pair(
    attention,
    residual,
    out_proj,
    gain_in,
    router,
    expert_ids,
    live_rows,
    expert_gate,
    expert_up,
    expert_down,
    shared_gate,
    shared_up,
    shared_down,
    gain_out,
):
    groups = 2
    experts = lax.axis_size("expert")
    me = lax.axis_index("dp")
    first = me == 0
    row_count = attention.shape[2]
    top_count = expert_ids.shape[3]
    capacity = max(2, (2 * row_count * top_count + experts - 1) // experts)
    gate_local = expert_gate[0]
    up_local = expert_up[0]
    down_local = expert_down[0]
    column_width = down_local.shape[1]
    rows_all = groups * row_count

    attention_mine = attention[0, 0]
    pieces = jnp.concatenate([attention_mine, swap_pair(attention_mine)], axis=0)
    product = jnp.dot(pieces, out_proj, preferred_element_type=jnp.float32).astype(jnp.bfloat16)
    projected = in_axis_order(first, product[:row_count], swap_pair(product[row_count:]), 1)
    stream_in = residual[0, 0].astype(jnp.float32) + projected.astype(jnp.float32)
    normal_rows = rms_scale(stream_in, gain_in).astype(jnp.bfloat16)
    column = jnp.concatenate([normal_rows, swap_pair(normal_rows)], axis=0)
    logit_part = jnp.dot(column, router, preferred_element_type=jnp.float32)
    logits = in_axis_order(first, logit_part, halves_swapped(swap_pair(logit_part)), 1)

    ids = expert_ids[0]
    ids_local = jnp.where(first, ids, ids[::-1])
    counts = live_rows[:, 0]
    counts_local = jnp.where(first, counts, counts[::-1])
    group_of_block = jnp.where(first, jnp.arange(groups), jnp.arange(groups)[::-1]).astype(jnp.int32)

    flat_experts = ids_local.reshape(rows_all, top_count)
    picked = jnp.take_along_axis(logits, flat_experts, axis=1)
    probabilities = jax.nn.softmax(picked, axis=1)
    row_live = (jnp.arange(row_count, dtype=jnp.int32)[None, :] < counts_local[:, None]).reshape(
        rows_all
    )
    slot_live = jnp.broadcast_to(row_live[:, None], (rows_all, top_count))
    weights = probabilities.astype(jnp.bfloat16) * slot_live.astype(jnp.bfloat16)
    block_experts = flat_experts.reshape(groups, row_count * top_count)
    block_live = slot_live.reshape(groups, row_count * top_count)
    onehot = (
        (block_experts[:, :, None] == jnp.arange(experts, dtype=jnp.int32)) & block_live[:, :, None]
    ).astype(jnp.int32)
    before = jnp.cumsum(onehot, axis=1) - onehot
    position = jnp.sum(before * onehot, axis=2)
    slot_total = experts * groups * capacity
    offsets = group_of_block[:, None] * capacity
    target = jnp.where(
        block_live, block_experts * (groups * capacity) + offsets + position, slot_total
    ).reshape(rows_all, top_count)
    slot_hit = target[:, :, None] == jnp.arange(slot_total, dtype=jnp.int32)[None, None, :]
    fill = jnp.any(slot_hit, axis=1).astype(jnp.bfloat16)
    outgoing = lax.dot_general(
        fill, column, (((0,), (0,)), ((), ())), preferred_element_type=jnp.float32
    ).astype(jnp.bfloat16).reshape(experts, groups * capacity, column.shape[1])
    slot_rows = lax.all_to_all(outgoing, "expert", split_axis=0, concat_axis=0, tiled=True)
    flattened = slot_rows.reshape(-1, slot_rows.shape[-1])
    gate_value = by_rows(flattened, gate_local)
    up_value = by_rows(flattened, up_local)
    hidden = (jax.nn.silu(gate_value) * up_value).astype(jnp.bfloat16)
    hidden_peer = swap_pair(hidden)
    shared_gate_value = by_rows(column, shared_gate)
    shared_up_value = by_rows(column, shared_up)
    shared_hidden = (jax.nn.silu(shared_gate_value) * shared_up_value).astype(jnp.bfloat16)
    shared_peer = halves_swapped(swap_pair(shared_hidden))

    unit_count = hidden.shape[1]
    down_blocks = down_local.reshape(groups, unit_count, column_width)
    shared_blocks = shared_down.reshape(groups, unit_count, column_width)
    down_mine = lax.dynamic_index_in_dim(down_blocks, me, 0, keepdims=False)
    down_peer = lax.dynamic_index_in_dim(down_blocks, 1 - me, 0, keepdims=False)
    shared_mine = lax.dynamic_index_in_dim(shared_blocks, me, 0, keepdims=False)
    shared_other = lax.dynamic_index_in_dim(shared_blocks, 1 - me, 0, keepdims=False)
    routed_total = jnp.dot(hidden, down_mine, preferred_element_type=jnp.float32) + jnp.dot(
        hidden_peer, down_peer, preferred_element_type=jnp.float32
    )
    shared = jnp.dot(shared_hidden, shared_mine, preferred_element_type=jnp.float32) + jnp.dot(
        shared_peer, shared_other, preferred_element_type=jnp.float32
    )
    expert_out = routed_total.astype(jnp.bfloat16).reshape(experts, groups * capacity, column_width)
    returned = lax.all_to_all(
        expert_out, "expert", split_axis=0, concat_axis=0, tiled=True
    ).reshape(slot_total, column_width)
    combine = jnp.sum(
        jnp.where(slot_hit, weights[:, :, None], jnp.zeros((), jnp.bfloat16)), axis=1
    ).astype(jnp.bfloat16)
    routed = jnp.dot(combine, returned, preferred_element_type=jnp.float32)
    combined = jnp.where(row_live[:, None], routed + shared, 0.0)
    summed = in_axis_order(first, combined[:row_count], swap_pair(combined[row_count:]), 1)
    stream_sum = stream_in + summed
    stream = stream_sum.astype(jnp.bfloat16)[None, None]
    normed = rms_scale(stream_sum, gain_out).astype(jnp.bfloat16)[None, None]
    return (stream, normed)


def shards(*args):
    if lax.axis_size("dp") == 2:
        return shards_pair(*args)
    return shards_general(*args)


def solution(mesh):
    placed = (
        P("expert", "dp", None, None),
        P("expert", "dp", None, None),
        P(None, "dp"),
        P(),
        P(None, "dp"),
        P("expert", None, None, None),
        P(None, "expert"),
        P("expert", "dp", None),
        P("expert", "dp", None),
        P("expert", None, "dp"),
        P("dp", None),
        P("dp", None),
        P(None, "dp"),
        P(),
    )
    return jax.shard_map(
        shards,
        mesh=mesh,
        in_specs=placed,
        out_specs=(P("expert", "dp", None, None), P("expert", "dp", None, None)),
        check_vma=False,
    )
```

```python
import jax
import jax.numpy as jnp
from jax import lax
from jax.sharding import PartitionSpec as P


def rms_scale(features, scale_gain):
    return (
        features
        * lax.rsqrt(jnp.mean(features * features, axis=-1, keepdims=True) + 1e-06)
        * scale_gain
    )


def by_rows(left, weight_rows):
    return lax.dot_general(
        left, weight_rows, (((1,), (1,)), ((), ())), preferred_element_type=jnp.float32
    )


def fill_slots(features, targets, slot_total, top_count):
    entries = jnp.arange(targets.shape[0], dtype=jnp.int32)
    source = jnp.full((slot_total,), -1, jnp.int32).at[targets].set(entries, mode="drop")
    chosen = jnp.take(features, jnp.maximum(source, 0) // top_count, axis=0)
    return jnp.where((source >= 0)[:, None], chosen, jnp.zeros_like(chosen))


def shards_general(
    attention,
    residual,
    out_proj,
    gain_in,
    router,
    expert_ids,
    live_rows,
    expert_gate,
    expert_up,
    expert_down,
    shared_gate,
    shared_up,
    shared_down,
    gain_out,
):
    groups = lax.axis_size("dp")
    experts = lax.axis_size("expert")
    row_count = attention.shape[2]
    feature_width = residual.shape[3]
    top_count = expert_ids.shape[3]
    capacity = max(2, (2 * row_count * top_count + experts - 1) // experts)
    gate_local = expert_gate[0]
    up_local = expert_up[0]
    down_local = expert_down[0]
    column_width = down_local.shape[1]
    pieces = lax.all_gather(attention, "dp", axis=1, tiled=True)
    flattened = pieces.reshape(-1, pieces.shape[-1])
    product = jnp.dot(flattened, out_proj, preferred_element_type=jnp.float32).astype(jnp.bfloat16)
    columns = product.reshape(pieces.shape[:-1] + (out_proj.shape[1],))
    projected = lax.all_to_all(columns, "dp", split_axis=1, concat_axis=3, tiled=True)[0, 0]
    stream_in = residual[0, 0].astype(jnp.float32) + projected.astype(jnp.float32)
    normal_rows = rms_scale(stream_in, gain_in).astype(jnp.bfloat16)
    column = lax.all_gather(normal_rows[None], "dp", axis=0, tiled=True).reshape(
        groups * row_count, feature_width
    )
    logit_part = jnp.dot(column, router, preferred_element_type=jnp.float32)
    logits = lax.all_gather(logit_part, "dp", axis=1, tiled=True)
    flat_experts = expert_ids[0].reshape(groups * row_count, top_count)
    picked = jnp.take_along_axis(logits, flat_experts, axis=1)
    probabilities = jax.nn.softmax(picked, axis=1)
    row_live = (jnp.arange(row_count, dtype=jnp.int32)[None, :] < live_rows[:, 0][:, None]).reshape(
        groups * row_count
    )
    slot_live = jnp.broadcast_to(row_live[:, None], (groups * row_count, top_count))
    weights = probabilities.astype(jnp.bfloat16) * slot_live.astype(jnp.bfloat16)
    block_experts = flat_experts.reshape(groups, row_count * top_count)
    block_live = slot_live.reshape(groups, row_count * top_count)
    onehot = (
        (block_experts[:, :, None] == jnp.arange(experts, dtype=jnp.int32)) & block_live[:, :, None]
    ).astype(jnp.int32)
    before = jnp.cumsum(onehot, axis=1) - onehot
    position = jnp.sum(before * onehot, axis=2)
    slot_total = experts * groups * capacity
    offsets = jnp.arange(groups, dtype=jnp.int32)[:, None] * capacity
    target = jnp.where(
        block_live, block_experts * (groups * capacity) + offsets + position, slot_total
    ).reshape(-1)
    outgoing = fill_slots(column, target, slot_total, top_count).reshape(
        experts, groups * capacity, feature_width
    )
    slot_rows = lax.all_to_all(outgoing, "expert", split_axis=0, concat_axis=0, tiled=True)
    flattened = slot_rows.reshape(-1, slot_rows.shape[-1])
    gate_value = by_rows(flattened, gate_local)
    up_value = by_rows(flattened, up_local)
    hidden = (jax.nn.silu(gate_value) * up_value).astype(jnp.bfloat16)
    routed_hidden = hidden.reshape(slot_rows.shape[:-1] + (gate_local.shape[0],))
    shared_gate_value = by_rows(column, shared_gate)
    shared_up_value = by_rows(column, shared_up)
    shared_hidden = (jax.nn.silu(shared_gate_value) * shared_up_value).astype(jnp.bfloat16)[None]
    routed_piece = lax.all_gather(routed_hidden, "dp", axis=2, tiled=True)
    shared_piece = lax.all_gather(shared_hidden, "dp", axis=2, tiled=True)
    count = routed_piece.shape[2]
    routed_total = jnp.dot(
        routed_piece.reshape(-1, count), down_local, preferred_element_type=jnp.float32
    )
    shared_total = jnp.dot(
        shared_piece.reshape(-1, shared_piece.shape[2]),
        shared_down,
        preferred_element_type=jnp.float32,
    )
    routed_total, shared = (routed_total, shared_total)
    expert_out = routed_total.astype(jnp.bfloat16).reshape(experts, groups * capacity, column_width)
    returned = lax.all_to_all(
        expert_out, "expert", split_axis=0, concat_axis=0, tiled=True
    ).reshape(slot_total, column_width)
    gathered = jnp.take(returned, jnp.minimum(target, slot_total - 1), axis=0).reshape(
        groups * row_count, top_count, column_width
    )
    routed = jnp.einsum("nk,nkd->nd", weights, gathered, preferred_element_type=jnp.float32)
    combined = jnp.where(row_live[:, None], routed + shared, 0.0).reshape(
        groups, row_count, column_width
    )
    summed = lax.all_to_all(combined, "dp", split_axis=0, concat_axis=2, tiled=True)[0]
    stream_sum = stream_in + summed
    stream = stream_sum.astype(jnp.bfloat16)[None, None]
    normed = rms_scale(stream_sum, gain_out).astype(jnp.bfloat16)[None, None]
    return (stream, normed)


def swap_pair(x):
    return lax.ppermute(x, "dp", [(0, 1), (1, 0)])


def halves_swapped(x):
    half = x.shape[0] // 2
    return jnp.concatenate([x[half:], x[:half]], axis=0)


def in_axis_order(first, mine, peer, axis):
    return jnp.where(
        first, jnp.concatenate([mine, peer], axis=axis), jnp.concatenate([peer, mine], axis=axis)
    )


def shards_pair(
    attention,
    residual,
    out_proj,
    gain_in,
    router,
    expert_ids,
    live_rows,
    expert_gate,
    expert_up,
    expert_down,
    shared_gate,
    shared_up,
    shared_down,
    gain_out,
):
    groups = 2
    experts = lax.axis_size("expert")
    me = lax.axis_index("dp")
    first = me == 0
    row_count = attention.shape[2]
    top_count = expert_ids.shape[3]
    capacity = max(2, (2 * row_count * top_count + experts - 1) // experts)
    gate_local = expert_gate[0]
    up_local = expert_up[0]
    down_local = expert_down[0]
    column_width = down_local.shape[1]
    rows_all = groups * row_count

    attention_mine = attention[0, 0]
    pieces = jnp.concatenate([attention_mine, swap_pair(attention_mine)], axis=0)
    product = jnp.dot(pieces, out_proj, preferred_element_type=jnp.float32).astype(jnp.bfloat16)
    projected = in_axis_order(first, product[:row_count], swap_pair(product[row_count:]), 1)
    stream_in = residual[0, 0].astype(jnp.float32) + projected.astype(jnp.float32)
    normal_rows = rms_scale(stream_in, gain_in).astype(jnp.bfloat16)
    column = jnp.concatenate([normal_rows, swap_pair(normal_rows)], axis=0)
    logit_part = jnp.dot(column, router, preferred_element_type=jnp.float32)
    logits = in_axis_order(first, logit_part, halves_swapped(swap_pair(logit_part)), 1)

    ids = expert_ids[0]
    ids_local = jnp.where(first, ids, ids[::-1])
    counts = live_rows[:, 0]
    counts_local = jnp.where(first, counts, counts[::-1])
    group_of_block = jnp.where(first, jnp.arange(groups), jnp.arange(groups)[::-1]).astype(jnp.int32)

    flat_experts = ids_local.reshape(rows_all, top_count)
    picked = jnp.take_along_axis(logits, flat_experts, axis=1)
    probabilities = jax.nn.softmax(picked, axis=1)
    row_live = (jnp.arange(row_count, dtype=jnp.int32)[None, :] < counts_local[:, None]).reshape(
        rows_all
    )
    slot_live = jnp.broadcast_to(row_live[:, None], (rows_all, top_count))
    weights = probabilities.astype(jnp.bfloat16) * slot_live.astype(jnp.bfloat16)
    block_experts = flat_experts.reshape(groups, row_count * top_count)
    block_live = slot_live.reshape(groups, row_count * top_count)
    onehot = (
        (block_experts[:, :, None] == jnp.arange(experts, dtype=jnp.int32)) & block_live[:, :, None]
    ).astype(jnp.int32)
    before = jnp.cumsum(onehot, axis=1) - onehot
    position = jnp.sum(before * onehot, axis=2)
    slot_total = experts * groups * capacity
    offsets = group_of_block[:, None] * capacity
    target = jnp.where(
        block_live, block_experts * (groups * capacity) + offsets + position, slot_total
    ).reshape(rows_all, top_count)
    slot_hit = target[:, :, None] == jnp.arange(slot_total, dtype=jnp.int32)[None, None, :]
    fill = jnp.any(slot_hit, axis=1).astype(jnp.bfloat16)
    outgoing = lax.dot_general(
        fill, column, (((0,), (0,)), ((), ())), preferred_element_type=jnp.float32
    ).astype(jnp.bfloat16).reshape(experts, groups * capacity, column.shape[1])
    slot_rows = lax.all_to_all(outgoing, "expert", split_axis=0, concat_axis=0, tiled=True)
    flattened = slot_rows.reshape(-1, slot_rows.shape[-1])
    unit_count = gate_local.shape[0]
    split = min(unit_count, 384) if unit_count > 384 else unit_count
    bounds = [(0, split)] + ([(split, unit_count)] if split < unit_count else [])
    down_blocks = down_local.reshape(groups, unit_count, column_width)
    down_mine = lax.dynamic_index_in_dim(down_blocks, me, 0, keepdims=False)
    down_peer = lax.dynamic_index_in_dim(down_blocks, 1 - me, 0, keepdims=False)
    chunks = []
    for low, high in bounds:
        gate_value = by_rows(flattened, gate_local[low:high])
        up_value = by_rows(flattened, up_local[low:high])
        hidden = (jax.nn.silu(gate_value) * up_value).astype(jnp.bfloat16)
        chunks.append((low, high, hidden, swap_pair(hidden)))
    shared_gate_value = by_rows(column, shared_gate)
    shared_up_value = by_rows(column, shared_up)
    shared_hidden = (jax.nn.silu(shared_gate_value) * shared_up_value).astype(jnp.bfloat16)
    shared_peer = halves_swapped(swap_pair(shared_hidden))

    routed_total = None
    for low, high, hidden, _ in chunks:
        part = jnp.dot(hidden, down_mine[low:high], preferred_element_type=jnp.float32)
        routed_total = part if routed_total is None else routed_total + part
    for low, high, _, hidden_peer in chunks:
        routed_total = routed_total + jnp.dot(
            hidden_peer, down_peer[low:high], preferred_element_type=jnp.float32
        )
    shared_blocks = shared_down.reshape(groups, shared_hidden.shape[1], column_width)
    shared_mine = lax.dynamic_index_in_dim(shared_blocks, me, 0, keepdims=False)
    shared_other = lax.dynamic_index_in_dim(shared_blocks, 1 - me, 0, keepdims=False)
    shared = jnp.dot(shared_hidden, shared_mine, preferred_element_type=jnp.float32) + jnp.dot(
        shared_peer, shared_other, preferred_element_type=jnp.float32
    )
    expert_out = routed_total.astype(jnp.bfloat16).reshape(experts, groups * capacity, column_width)
    returned = lax.all_to_all(
        expert_out, "expert", split_axis=0, concat_axis=0, tiled=True
    ).reshape(slot_total, column_width)
    combine = jnp.sum(
        jnp.where(slot_hit, weights[:, :, None], jnp.zeros((), jnp.bfloat16)), axis=1
    ).astype(jnp.bfloat16)
    routed = jnp.dot(combine, returned, preferred_element_type=jnp.float32)
    combined = jnp.where(row_live[:, None], routed + shared, 0.0)
    summed = in_axis_order(first, combined[:row_count], swap_pair(combined[row_count:]), 1)
    stream_sum = stream_in + summed
    stream = stream_sum.astype(jnp.bfloat16)[None, None]
    normed = rms_scale(stream_sum, gain_out).astype(jnp.bfloat16)[None, None]
    return (stream, normed)


def shards(*args):
    if lax.axis_size("dp") == 2:
        return shards_pair(*args)
    return shards_general(*args)


def solution(mesh):
    placed = (
        P("expert", "dp", None, None),
        P("expert", "dp", None, None),
        P(None, "dp"),
        P(),
        P(None, "dp"),
        P("expert", None, None, None),
        P(None, "expert"),
        P("expert", "dp", None),
        P("expert", "dp", None),
        P("expert", None, "dp"),
        P("dp", None),
        P("dp", None),
        P(None, "dp"),
        P(),
    )
    return jax.shard_map(
        shards,
        mesh=mesh,
        in_specs=placed,
        out_specs=(P("expert", "dp", None, None), P("expert", "dp", None, None)),
        check_vma=False,
    )
```

```python
import jax
import jax.numpy as jnp
from jax import lax
from jax.sharding import PartitionSpec as P


def rms_scale(features, scale_gain):
    return (
        features
        * lax.rsqrt(jnp.mean(features * features, axis=-1, keepdims=True) + 1e-06)
        * scale_gain
    )


def by_rows(left, weight_rows):
    return lax.dot_general(
        left, weight_rows, (((1,), (1,)), ((), ())), preferred_element_type=jnp.float32
    )


def fill_slots(features, targets, slot_total, top_count):
    entries = jnp.arange(targets.shape[0], dtype=jnp.int32)
    source = jnp.full((slot_total,), -1, jnp.int32).at[targets].set(entries, mode="drop")
    chosen = jnp.take(features, jnp.maximum(source, 0) // top_count, axis=0)
    return jnp.where((source >= 0)[:, None], chosen, jnp.zeros_like(chosen))


def shards_general(
    attention,
    residual,
    out_proj,
    gain_in,
    router,
    expert_ids,
    live_rows,
    expert_gate,
    expert_up,
    expert_down,
    shared_gate,
    shared_up,
    shared_down,
    gain_out,
):
    groups = lax.axis_size("dp")
    experts = lax.axis_size("expert")
    row_count = attention.shape[2]
    feature_width = residual.shape[3]
    top_count = expert_ids.shape[3]
    capacity = max(2, (2 * row_count * top_count + experts - 1) // experts)
    gate_local = expert_gate[0]
    up_local = expert_up[0]
    down_local = expert_down[0]
    column_width = down_local.shape[1]
    pieces = lax.all_gather(attention, "dp", axis=1, tiled=True)
    flattened = pieces.reshape(-1, pieces.shape[-1])
    product = jnp.dot(flattened, out_proj, preferred_element_type=jnp.float32).astype(jnp.bfloat16)
    columns = product.reshape(pieces.shape[:-1] + (out_proj.shape[1],))
    projected = lax.all_to_all(columns, "dp", split_axis=1, concat_axis=3, tiled=True)[0, 0]
    stream_in = residual[0, 0].astype(jnp.float32) + projected.astype(jnp.float32)
    normal_rows = rms_scale(stream_in, gain_in).astype(jnp.bfloat16)
    column = lax.all_gather(normal_rows[None], "dp", axis=0, tiled=True).reshape(
        groups * row_count, feature_width
    )
    logit_part = jnp.dot(column, router, preferred_element_type=jnp.float32)
    logits = lax.all_gather(logit_part, "dp", axis=1, tiled=True)
    flat_experts = expert_ids[0].reshape(groups * row_count, top_count)
    picked = jnp.take_along_axis(logits, flat_experts, axis=1)
    probabilities = jax.nn.softmax(picked, axis=1)
    row_live = (jnp.arange(row_count, dtype=jnp.int32)[None, :] < live_rows[:, 0][:, None]).reshape(
        groups * row_count
    )
    slot_live = jnp.broadcast_to(row_live[:, None], (groups * row_count, top_count))
    weights = probabilities.astype(jnp.bfloat16) * slot_live.astype(jnp.bfloat16)
    block_experts = flat_experts.reshape(groups, row_count * top_count)
    block_live = slot_live.reshape(groups, row_count * top_count)
    onehot = (
        (block_experts[:, :, None] == jnp.arange(experts, dtype=jnp.int32)) & block_live[:, :, None]
    ).astype(jnp.int32)
    before = jnp.cumsum(onehot, axis=1) - onehot
    position = jnp.sum(before * onehot, axis=2)
    slot_total = experts * groups * capacity
    offsets = jnp.arange(groups, dtype=jnp.int32)[:, None] * capacity
    target = jnp.where(
        block_live, block_experts * (groups * capacity) + offsets + position, slot_total
    ).reshape(-1)
    outgoing = fill_slots(column, target, slot_total, top_count).reshape(
        experts, groups * capacity, feature_width
    )
    slot_rows = lax.all_to_all(outgoing, "expert", split_axis=0, concat_axis=0, tiled=True)
    flattened = slot_rows.reshape(-1, slot_rows.shape[-1])
    gate_value = by_rows(flattened, gate_local)
    up_value = by_rows(flattened, up_local)
    hidden = (jax.nn.silu(gate_value) * up_value).astype(jnp.bfloat16)
    routed_hidden = hidden.reshape(slot_rows.shape[:-1] + (gate_local.shape[0],))
    shared_gate_value = by_rows(column, shared_gate)
    shared_up_value = by_rows(column, shared_up)
    shared_hidden = (jax.nn.silu(shared_gate_value) * shared_up_value).astype(jnp.bfloat16)[None]
    routed_piece = lax.all_gather(routed_hidden, "dp", axis=2, tiled=True)
    shared_piece = lax.all_gather(shared_hidden, "dp", axis=2, tiled=True)
    count = routed_piece.shape[2]
    routed_total = jnp.dot(
        routed_piece.reshape(-1, count), down_local, preferred_element_type=jnp.float32
    )
    shared_total = jnp.dot(
        shared_piece.reshape(-1, shared_piece.shape[2]),
        shared_down,
        preferred_element_type=jnp.float32,
    )
    routed_total, shared = (routed_total, shared_total)
    expert_out = routed_total.astype(jnp.bfloat16).reshape(experts, groups * capacity, column_width)
    returned = lax.all_to_all(
        expert_out, "expert", split_axis=0, concat_axis=0, tiled=True
    ).reshape(slot_total, column_width)
    gathered = jnp.take(returned, jnp.minimum(target, slot_total - 1), axis=0).reshape(
        groups * row_count, top_count, column_width
    )
    routed = jnp.einsum("nk,nkd->nd", weights, gathered, preferred_element_type=jnp.float32)
    combined = jnp.where(row_live[:, None], routed + shared, 0.0).reshape(
        groups, row_count, column_width
    )
    summed = lax.all_to_all(combined, "dp", split_axis=0, concat_axis=2, tiled=True)[0]
    stream_sum = stream_in + summed
    stream = stream_sum.astype(jnp.bfloat16)[None, None]
    normed = rms_scale(stream_sum, gain_out).astype(jnp.bfloat16)[None, None]
    return (stream, normed)


def swap_pair(x):
    return lax.ppermute(x, "dp", [(0, 1), (1, 0)])


def halves_swapped(x):
    half = x.shape[0] // 2
    return jnp.concatenate([x[half:], x[:half]], axis=0)


def in_axis_order(first, mine, peer, axis):
    return jnp.where(
        first, jnp.concatenate([mine, peer], axis=axis), jnp.concatenate([peer, mine], axis=axis)
    )


def shards_pair(
    attention,
    residual,
    out_proj,
    gain_in,
    router,
    expert_ids,
    live_rows,
    expert_gate,
    expert_up,
    expert_down,
    shared_gate,
    shared_up,
    shared_down,
    gain_out,
):
    groups = 2
    experts = lax.axis_size("expert")
    me = lax.axis_index("dp")
    first = me == 0
    row_count = attention.shape[2]
    top_count = expert_ids.shape[3]
    capacity = max(2, (2 * row_count * top_count + experts - 1) // experts)
    gate_local = expert_gate[0]
    up_local = expert_up[0]
    down_local = expert_down[0]
    column_width = down_local.shape[1]
    rows_all = groups * row_count

    attention_mine = attention[0, 0]
    residual_mine = residual[0, 0]
    pieces = jnp.concatenate([attention_mine, swap_pair(attention_mine)], axis=0)
    residual_all = jnp.concatenate([residual_mine, swap_pair(residual_mine)], axis=0)
    product = jnp.dot(pieces, out_proj, preferred_element_type=jnp.float32).astype(jnp.bfloat16)
    projected = in_axis_order(first, product, halves_swapped(swap_pair(product)), 1)
    stream_all = residual_all.astype(jnp.float32) + projected.astype(jnp.float32)
    column = rms_scale(stream_all, gain_in).astype(jnp.bfloat16)
    stream_in = stream_all[:row_count]
    logit_part = jnp.dot(column, router, preferred_element_type=jnp.float32)
    logits = in_axis_order(first, logit_part, halves_swapped(swap_pair(logit_part)), 1)

    ids = expert_ids[0]
    ids_local = jnp.where(first, ids, ids[::-1])
    counts = live_rows[:, 0]
    counts_local = jnp.where(first, counts, counts[::-1])
    group_of_block = jnp.where(first, jnp.arange(groups), jnp.arange(groups)[::-1]).astype(jnp.int32)

    flat_experts = ids_local.reshape(rows_all, top_count)
    picked = jnp.take_along_axis(logits, flat_experts, axis=1)
    probabilities = jax.nn.softmax(picked, axis=1)
    row_live = (jnp.arange(row_count, dtype=jnp.int32)[None, :] < counts_local[:, None]).reshape(
        rows_all
    )
    slot_live = jnp.broadcast_to(row_live[:, None], (rows_all, top_count))
    weights = probabilities.astype(jnp.bfloat16) * slot_live.astype(jnp.bfloat16)
    block_experts = flat_experts.reshape(groups, row_count * top_count)
    block_live = slot_live.reshape(groups, row_count * top_count)
    onehot = (
        (block_experts[:, :, None] == jnp.arange(experts, dtype=jnp.int32)) & block_live[:, :, None]
    ).astype(jnp.int32)
    before = jnp.cumsum(onehot, axis=1) - onehot
    position = jnp.sum(before * onehot, axis=2)
    slot_total = experts * groups * capacity
    offsets = group_of_block[:, None] * capacity
    target = jnp.where(
        block_live, block_experts * (groups * capacity) + offsets + position, slot_total
    ).reshape(rows_all, top_count)
    slot_hit = target[:, :, None] == jnp.arange(slot_total, dtype=jnp.int32)[None, None, :]
    fill = jnp.any(slot_hit, axis=1).astype(jnp.bfloat16)
    outgoing = lax.dot_general(
        fill, column, (((0,), (0,)), ((), ())), preferred_element_type=jnp.float32
    ).astype(jnp.bfloat16).reshape(experts, groups * capacity, column.shape[1])
    slot_rows = lax.all_to_all(outgoing, "expert", split_axis=0, concat_axis=0, tiled=True)
    flattened = slot_rows.reshape(-1, slot_rows.shape[-1])
    gate_value = by_rows(flattened, gate_local)
    up_value = by_rows(flattened, up_local)
    hidden = (jax.nn.silu(gate_value) * up_value).astype(jnp.bfloat16)
    hidden_peer = swap_pair(hidden)
    shared_gate_value = by_rows(column, shared_gate)
    shared_up_value = by_rows(column, shared_up)
    shared_hidden = (jax.nn.silu(shared_gate_value) * shared_up_value).astype(jnp.bfloat16)
    shared_peer = halves_swapped(swap_pair(shared_hidden))

    unit_count = hidden.shape[1]
    down_blocks = down_local.reshape(groups, unit_count, column_width)
    shared_blocks = shared_down.reshape(groups, unit_count, column_width)
    down_mine = lax.dynamic_index_in_dim(down_blocks, me, 0, keepdims=False)
    down_peer = lax.dynamic_index_in_dim(down_blocks, 1 - me, 0, keepdims=False)
    shared_mine = lax.dynamic_index_in_dim(shared_blocks, me, 0, keepdims=False)
    shared_other = lax.dynamic_index_in_dim(shared_blocks, 1 - me, 0, keepdims=False)
    routed_total = jnp.dot(hidden, down_mine, preferred_element_type=jnp.float32) + jnp.dot(
        hidden_peer, down_peer, preferred_element_type=jnp.float32
    )
    shared = jnp.dot(shared_hidden, shared_mine, preferred_element_type=jnp.float32) + jnp.dot(
        shared_peer, shared_other, preferred_element_type=jnp.float32
    )
    expert_out = routed_total.astype(jnp.bfloat16).reshape(experts, groups * capacity, column_width)
    returned = lax.all_to_all(
        expert_out, "expert", split_axis=0, concat_axis=0, tiled=True
    ).reshape(slot_total, column_width)
    combine = jnp.sum(
        jnp.where(slot_hit, weights[:, :, None], jnp.zeros((), jnp.bfloat16)), axis=1
    ).astype(jnp.bfloat16)
    routed = jnp.dot(combine, returned, preferred_element_type=jnp.float32)
    combined = jnp.where(row_live[:, None], routed + shared, 0.0)
    summed = in_axis_order(first, combined[:row_count], swap_pair(combined[row_count:]), 1)
    stream_sum = stream_in + summed
    stream = stream_sum.astype(jnp.bfloat16)[None, None]
    normed = rms_scale(stream_sum, gain_out).astype(jnp.bfloat16)[None, None]
    return (stream, normed)


def shards(*args):
    if lax.axis_size("dp") == 2:
        return shards_pair(*args)
    return shards_general(*args)


def solution(mesh):
    placed = (
        P("expert", "dp", None, None),
        P("expert", "dp", None, None),
        P(None, "dp"),
        P(),
        P(None, "dp"),
        P("expert", None, None, None),
        P(None, "expert"),
        P("expert", "dp", None),
        P("expert", "dp", None),
        P("expert", None, "dp"),
        P("dp", None),
        P("dp", None),
        P(None, "dp"),
        P(),
    )
    return jax.shard_map(
        shards,
        mesh=mesh,
        in_specs=placed,
        out_specs=(P("expert", "dp", None, None), P("expert", "dp", None, None)),
        check_vma=False,
    )
```

```python
import jax
import jax.numpy as jnp
from jax import lax
from jax.experimental import pallas as pl
from jax.experimental.pallas import tpu as pltpu
from jax.sharding import PartitionSpec as P


def rms_scale(features, scale_gain):
    return (
        features
        * lax.rsqrt(jnp.mean(features * features, axis=-1, keepdims=True) + 1e-06)
        * scale_gain
    )


def by_rows(left, weight_rows):
    return lax.dot_general(
        left, weight_rows, (((1,), (1,)), ((), ())), preferred_element_type=jnp.float32
    )


def fill_slots(features, targets, slot_total, top_count):
    entries = jnp.arange(targets.shape[0], dtype=jnp.int32)
    source = jnp.full((slot_total,), -1, jnp.int32).at[targets].set(entries, mode="drop")
    chosen = jnp.take(features, jnp.maximum(source, 0) // top_count, axis=0)
    return jnp.where((source >= 0)[:, None], chosen, jnp.zeros_like(chosen))


def shards_general(
    attention,
    residual,
    out_proj,
    gain_in,
    router,
    expert_ids,
    live_rows,
    expert_gate,
    expert_up,
    expert_down,
    shared_gate,
    shared_up,
    shared_down,
    gain_out,
):
    groups = lax.axis_size("dp")
    experts = lax.axis_size("expert")
    row_count = attention.shape[2]
    feature_width = residual.shape[3]
    top_count = expert_ids.shape[3]
    capacity = max(2, (2 * row_count * top_count + experts - 1) // experts)
    gate_local = expert_gate[0]
    up_local = expert_up[0]
    down_local = expert_down[0]
    column_width = down_local.shape[1]
    pieces = lax.all_gather(attention, "dp", axis=1, tiled=True)
    flattened = pieces.reshape(-1, pieces.shape[-1])
    product = jnp.dot(flattened, out_proj, preferred_element_type=jnp.float32).astype(jnp.bfloat16)
    columns = product.reshape(pieces.shape[:-1] + (out_proj.shape[1],))
    projected = lax.all_to_all(columns, "dp", split_axis=1, concat_axis=3, tiled=True)[0, 0]
    stream_in = residual[0, 0].astype(jnp.float32) + projected.astype(jnp.float32)
    normal_rows = rms_scale(stream_in, gain_in).astype(jnp.bfloat16)
    column = lax.all_gather(normal_rows[None], "dp", axis=0, tiled=True).reshape(
        groups * row_count, feature_width
    )
    logit_part = jnp.dot(column, router, preferred_element_type=jnp.float32)
    logits = lax.all_gather(logit_part, "dp", axis=1, tiled=True)
    flat_experts = expert_ids[0].reshape(groups * row_count, top_count)
    picked = jnp.take_along_axis(logits, flat_experts, axis=1)
    probabilities = jax.nn.softmax(picked, axis=1)
    row_live = (jnp.arange(row_count, dtype=jnp.int32)[None, :] < live_rows[:, 0][:, None]).reshape(
        groups * row_count
    )
    slot_live = jnp.broadcast_to(row_live[:, None], (groups * row_count, top_count))
    weights = probabilities.astype(jnp.bfloat16) * slot_live.astype(jnp.bfloat16)
    block_experts = flat_experts.reshape(groups, row_count * top_count)
    block_live = slot_live.reshape(groups, row_count * top_count)
    onehot = (
        (block_experts[:, :, None] == jnp.arange(experts, dtype=jnp.int32)) & block_live[:, :, None]
    ).astype(jnp.int32)
    before = jnp.cumsum(onehot, axis=1) - onehot
    position = jnp.sum(before * onehot, axis=2)
    slot_total = experts * groups * capacity
    offsets = jnp.arange(groups, dtype=jnp.int32)[:, None] * capacity
    target = jnp.where(
        block_live, block_experts * (groups * capacity) + offsets + position, slot_total
    ).reshape(-1)
    outgoing = fill_slots(column, target, slot_total, top_count).reshape(
        experts, groups * capacity, feature_width
    )
    slot_rows = lax.all_to_all(outgoing, "expert", split_axis=0, concat_axis=0, tiled=True)
    flattened = slot_rows.reshape(-1, slot_rows.shape[-1])
    gate_value = by_rows(flattened, gate_local)
    up_value = by_rows(flattened, up_local)
    hidden = (jax.nn.silu(gate_value) * up_value).astype(jnp.bfloat16)
    routed_hidden = hidden.reshape(slot_rows.shape[:-1] + (gate_local.shape[0],))
    shared_gate_value = by_rows(column, shared_gate)
    shared_up_value = by_rows(column, shared_up)
    shared_hidden = (jax.nn.silu(shared_gate_value) * shared_up_value).astype(jnp.bfloat16)[None]
    routed_piece = lax.all_gather(routed_hidden, "dp", axis=2, tiled=True)
    shared_piece = lax.all_gather(shared_hidden, "dp", axis=2, tiled=True)
    count = routed_piece.shape[2]
    routed_total = jnp.dot(
        routed_piece.reshape(-1, count), down_local, preferred_element_type=jnp.float32
    )
    shared_total = jnp.dot(
        shared_piece.reshape(-1, shared_piece.shape[2]),
        shared_down,
        preferred_element_type=jnp.float32,
    )
    routed_total, shared = (routed_total, shared_total)
    expert_out = routed_total.astype(jnp.bfloat16).reshape(experts, groups * capacity, column_width)
    returned = lax.all_to_all(
        expert_out, "expert", split_axis=0, concat_axis=0, tiled=True
    ).reshape(slot_total, column_width)
    gathered = jnp.take(returned, jnp.minimum(target, slot_total - 1), axis=0).reshape(
        groups * row_count, top_count, column_width
    )
    routed = jnp.einsum("nk,nkd->nd", weights, gathered, preferred_element_type=jnp.float32)
    combined = jnp.where(row_live[:, None], routed + shared, 0.0).reshape(
        groups, row_count, column_width
    )
    summed = lax.all_to_all(combined, "dp", split_axis=0, concat_axis=2, tiled=True)[0]
    stream_sum = stream_in + summed
    stream = stream_sum.astype(jnp.bfloat16)[None, None]
    normed = rms_scale(stream_sum, gain_out).astype(jnp.bfloat16)[None, None]
    return (stream, normed)


def gate_up_kernel(rows_ref, gate_ref, up_ref, hidden_ref):
    rows = rows_ref[...]
    contract = (((1,), (1,)), ((), ()))
    gate_value = lax.dot_general(rows, gate_ref[...], contract, preferred_element_type=jnp.float32)
    up_value = lax.dot_general(rows, up_ref[...], contract, preferred_element_type=jnp.float32)
    silu = gate_value / (1.0 + jnp.exp(-gate_value))
    hidden_ref[...] = (silu * up_value).astype(hidden_ref.dtype)


def gate_up(rows, gate_weight, up_weight):
    count, width = rows.shape
    units = gate_weight.shape[0]
    in_vmem = pl.BlockSpec(memory_space=pltpu.VMEM)
    return pl.pallas_call(
        gate_up_kernel,
        out_shape=jax.ShapeDtypeStruct((count, units), jnp.bfloat16),
        in_specs=[in_vmem, in_vmem, in_vmem],
        out_specs=in_vmem,
        cost_estimate=pl.CostEstimate(
            flops=4 * count * width * units,
            transcendentals=count * units,
            bytes_accessed=2 * (count * width + 2 * units * width + count * units),
        ),
    )(rows, gate_weight, up_weight)


def swap_pair(x):
    return lax.ppermute(x, "dp", [(0, 1), (1, 0)])


def halves_swapped(x):
    half = x.shape[0] // 2
    return jnp.concatenate([x[half:], x[:half]], axis=0)


def in_axis_order(first, mine, peer, axis):
    return jnp.where(
        first, jnp.concatenate([mine, peer], axis=axis), jnp.concatenate([peer, mine], axis=axis)
    )


def shards_pair(
    attention,
    residual,
    out_proj,
    gain_in,
    router,
    expert_ids,
    live_rows,
    expert_gate,
    expert_up,
    expert_down,
    shared_gate,
    shared_up,
    shared_down,
    gain_out,
):
    groups = 2
    experts = lax.axis_size("expert")
    me = lax.axis_index("dp")
    first = me == 0
    row_count = attention.shape[2]
    top_count = expert_ids.shape[3]
    capacity = max(2, (2 * row_count * top_count + experts - 1) // experts)
    gate_local = expert_gate[0]
    up_local = expert_up[0]
    down_local = expert_down[0]
    column_width = down_local.shape[1]
    rows_all = groups * row_count

    attention_mine = attention[0, 0]
    residual_mine = residual[0, 0]
    pieces = jnp.concatenate([attention_mine, swap_pair(attention_mine)], axis=0)
    residual_all = jnp.concatenate([residual_mine, swap_pair(residual_mine)], axis=0)
    product = jnp.dot(pieces, out_proj, preferred_element_type=jnp.float32).astype(jnp.bfloat16)
    projected = in_axis_order(first, product, halves_swapped(swap_pair(product)), 1)
    stream_all = residual_all.astype(jnp.float32) + projected.astype(jnp.float32)
    column = rms_scale(stream_all, gain_in).astype(jnp.bfloat16)
    stream_in = stream_all[:row_count]
    logit_part = jnp.dot(column, router, preferred_element_type=jnp.float32)
    logits = in_axis_order(first, logit_part, halves_swapped(swap_pair(logit_part)), 1)

    ids = expert_ids[0]
    ids_local = jnp.where(first, ids, ids[::-1])
    counts = live_rows[:, 0]
    counts_local = jnp.where(first, counts, counts[::-1])
    group_of_block = jnp.where(first, jnp.arange(groups), jnp.arange(groups)[::-1]).astype(jnp.int32)

    flat_experts = ids_local.reshape(rows_all, top_count)
    picked = jnp.take_along_axis(logits, flat_experts, axis=1)
    probabilities = jax.nn.softmax(picked, axis=1)
    row_live = (jnp.arange(row_count, dtype=jnp.int32)[None, :] < counts_local[:, None]).reshape(
        rows_all
    )
    slot_live = jnp.broadcast_to(row_live[:, None], (rows_all, top_count))
    weights = probabilities.astype(jnp.bfloat16) * slot_live.astype(jnp.bfloat16)
    block_experts = flat_experts.reshape(groups, row_count * top_count)
    block_live = slot_live.reshape(groups, row_count * top_count)
    onehot = (
        (block_experts[:, :, None] == jnp.arange(experts, dtype=jnp.int32)) & block_live[:, :, None]
    ).astype(jnp.int32)
    before = jnp.cumsum(onehot, axis=1) - onehot
    position = jnp.sum(before * onehot, axis=2)
    slot_total = experts * groups * capacity
    offsets = group_of_block[:, None] * capacity
    target = jnp.where(
        block_live, block_experts * (groups * capacity) + offsets + position, slot_total
    ).reshape(rows_all, top_count)
    slot_hit = target[:, :, None] == jnp.arange(slot_total, dtype=jnp.int32)[None, None, :]
    fill = jnp.any(slot_hit, axis=1).astype(jnp.bfloat16)
    outgoing = lax.dot_general(
        fill, column, (((0,), (0,)), ((), ())), preferred_element_type=jnp.float32
    ).astype(jnp.bfloat16).reshape(experts, groups * capacity, column.shape[1])
    slot_rows = lax.all_to_all(outgoing, "expert", split_axis=0, concat_axis=0, tiled=True)
    flattened = slot_rows.reshape(-1, slot_rows.shape[-1])
    hidden = gate_up(flattened, gate_local, up_local)
    hidden_peer = swap_pair(hidden)
    shared_gate_value = by_rows(column, shared_gate)
    shared_up_value = by_rows(column, shared_up)
    shared_hidden = (jax.nn.silu(shared_gate_value) * shared_up_value).astype(jnp.bfloat16)
    shared_peer = halves_swapped(swap_pair(shared_hidden))

    unit_count = hidden.shape[1]
    down_blocks = down_local.reshape(groups, unit_count, column_width)
    shared_blocks = shared_down.reshape(groups, unit_count, column_width)
    down_mine = lax.dynamic_index_in_dim(down_blocks, me, 0, keepdims=False)
    down_peer = lax.dynamic_index_in_dim(down_blocks, 1 - me, 0, keepdims=False)
    shared_mine = lax.dynamic_index_in_dim(shared_blocks, me, 0, keepdims=False)
    shared_other = lax.dynamic_index_in_dim(shared_blocks, 1 - me, 0, keepdims=False)
    routed_total = jnp.dot(hidden, down_mine, preferred_element_type=jnp.float32) + jnp.dot(
        hidden_peer, down_peer, preferred_element_type=jnp.float32
    )
    shared = jnp.dot(shared_hidden, shared_mine, preferred_element_type=jnp.float32) + jnp.dot(
        shared_peer, shared_other, preferred_element_type=jnp.float32
    )
    expert_out = routed_total.astype(jnp.bfloat16).reshape(experts, groups * capacity, column_width)
    returned = lax.all_to_all(
        expert_out, "expert", split_axis=0, concat_axis=0, tiled=True
    ).reshape(slot_total, column_width)
    combine = jnp.sum(
        jnp.where(slot_hit, weights[:, :, None], jnp.zeros((), jnp.bfloat16)), axis=1
    ).astype(jnp.bfloat16)
    routed = jnp.dot(combine, returned, preferred_element_type=jnp.float32)
    combined = jnp.where(row_live[:, None], routed + shared, 0.0)
    summed = in_axis_order(first, combined[:row_count], swap_pair(combined[row_count:]), 1)
    stream_sum = stream_in + summed
    stream = stream_sum.astype(jnp.bfloat16)[None, None]
    normed = rms_scale(stream_sum, gain_out).astype(jnp.bfloat16)[None, None]
    return (stream, normed)


def shards(*args):
    if lax.axis_size("dp") == 2:
        return shards_pair(*args)
    return shards_general(*args)


def solution(mesh):
    placed = (
        P("expert", "dp", None, None),
        P("expert", "dp", None, None),
        P(None, "dp"),
        P(),
        P(None, "dp"),
        P("expert", None, None, None),
        P(None, "expert"),
        P("expert", "dp", None),
        P("expert", "dp", None),
        P("expert", None, "dp"),
        P("dp", None),
        P("dp", None),
        P(None, "dp"),
        P(),
    )
    return jax.shard_map(
        shards,
        mesh=mesh,
        in_specs=placed,
        out_specs=(P("expert", "dp", None, None), P("expert", "dp", None, None)),
        check_vma=False,
    )
```

```python
import jax
import jax.numpy as jnp
from jax import lax
from jax.sharding import PartitionSpec as P


def rms_scale(features, scale_gain):
    return (
        features
        * lax.rsqrt(jnp.mean(features * features, axis=-1, keepdims=True) + 1e-06)
        * scale_gain
    )


def by_rows(left, weight_rows):
    return lax.dot_general(
        left, weight_rows, (((1,), (1,)), ((), ())), preferred_element_type=jnp.float32
    )


def fill_slots(features, targets, slot_total, top_count):
    entries = jnp.arange(targets.shape[0], dtype=jnp.int32)
    source = jnp.full((slot_total,), -1, jnp.int32).at[targets].set(entries, mode="drop")
    chosen = jnp.take(features, jnp.maximum(source, 0) // top_count, axis=0)
    return jnp.where((source >= 0)[:, None], chosen, jnp.zeros_like(chosen))


def shards_general(
    attention,
    residual,
    out_proj,
    gain_in,
    router,
    expert_ids,
    live_rows,
    expert_gate,
    expert_up,
    expert_down,
    shared_gate,
    shared_up,
    shared_down,
    gain_out,
):
    groups = lax.axis_size("dp")
    experts = lax.axis_size("expert")
    row_count = attention.shape[2]
    feature_width = residual.shape[3]
    top_count = expert_ids.shape[3]
    capacity = max(2, (2 * row_count * top_count + experts - 1) // experts)
    gate_local = expert_gate[0]
    up_local = expert_up[0]
    down_local = expert_down[0]
    column_width = down_local.shape[1]
    pieces = lax.all_gather(attention, "dp", axis=1, tiled=True)
    flattened = pieces.reshape(-1, pieces.shape[-1])
    product = jnp.dot(flattened, out_proj, preferred_element_type=jnp.float32).astype(jnp.bfloat16)
    columns = product.reshape(pieces.shape[:-1] + (out_proj.shape[1],))
    projected = lax.all_to_all(columns, "dp", split_axis=1, concat_axis=3, tiled=True)[0, 0]
    stream_in = residual[0, 0].astype(jnp.float32) + projected.astype(jnp.float32)
    normal_rows = rms_scale(stream_in, gain_in).astype(jnp.bfloat16)
    column = lax.all_gather(normal_rows[None], "dp", axis=0, tiled=True).reshape(
        groups * row_count, feature_width
    )
    logit_part = jnp.dot(column, router, preferred_element_type=jnp.float32)
    logits = lax.all_gather(logit_part, "dp", axis=1, tiled=True)
    flat_experts = expert_ids[0].reshape(groups * row_count, top_count)
    picked = jnp.take_along_axis(logits, flat_experts, axis=1)
    probabilities = jax.nn.softmax(picked, axis=1)
    row_live = (jnp.arange(row_count, dtype=jnp.int32)[None, :] < live_rows[:, 0][:, None]).reshape(
        groups * row_count
    )
    slot_live = jnp.broadcast_to(row_live[:, None], (groups * row_count, top_count))
    weights = probabilities.astype(jnp.bfloat16) * slot_live.astype(jnp.bfloat16)
    block_experts = flat_experts.reshape(groups, row_count * top_count)
    block_live = slot_live.reshape(groups, row_count * top_count)
    onehot = (
        (block_experts[:, :, None] == jnp.arange(experts, dtype=jnp.int32)) & block_live[:, :, None]
    ).astype(jnp.int32)
    before = jnp.cumsum(onehot, axis=1) - onehot
    position = jnp.sum(before * onehot, axis=2)
    slot_total = experts * groups * capacity
    offsets = jnp.arange(groups, dtype=jnp.int32)[:, None] * capacity
    target = jnp.where(
        block_live, block_experts * (groups * capacity) + offsets + position, slot_total
    ).reshape(-1)
    outgoing = fill_slots(column, target, slot_total, top_count).reshape(
        experts, groups * capacity, feature_width
    )
    slot_rows = lax.all_to_all(outgoing, "expert", split_axis=0, concat_axis=0, tiled=True)
    flattened = slot_rows.reshape(-1, slot_rows.shape[-1])
    gate_value = by_rows(flattened, gate_local)
    up_value = by_rows(flattened, up_local)
    hidden = (jax.nn.silu(gate_value) * up_value).astype(jnp.bfloat16)
    routed_hidden = hidden.reshape(slot_rows.shape[:-1] + (gate_local.shape[0],))
    shared_gate_value = by_rows(column, shared_gate)
    shared_up_value = by_rows(column, shared_up)
    shared_hidden = (jax.nn.silu(shared_gate_value) * shared_up_value).astype(jnp.bfloat16)[None]
    routed_piece = lax.all_gather(routed_hidden, "dp", axis=2, tiled=True)
    shared_piece = lax.all_gather(shared_hidden, "dp", axis=2, tiled=True)
    count = routed_piece.shape[2]
    routed_total = jnp.dot(
        routed_piece.reshape(-1, count), down_local, preferred_element_type=jnp.float32
    )
    shared_total = jnp.dot(
        shared_piece.reshape(-1, shared_piece.shape[2]),
        shared_down,
        preferred_element_type=jnp.float32,
    )
    routed_total, shared = (routed_total, shared_total)
    expert_out = routed_total.astype(jnp.bfloat16).reshape(experts, groups * capacity, column_width)
    returned = lax.all_to_all(
        expert_out, "expert", split_axis=0, concat_axis=0, tiled=True
    ).reshape(slot_total, column_width)
    gathered = jnp.take(returned, jnp.minimum(target, slot_total - 1), axis=0).reshape(
        groups * row_count, top_count, column_width
    )
    routed = jnp.einsum("nk,nkd->nd", weights, gathered, preferred_element_type=jnp.float32)
    combined = jnp.where(row_live[:, None], routed + shared, 0.0).reshape(
        groups, row_count, column_width
    )
    summed = lax.all_to_all(combined, "dp", split_axis=0, concat_axis=2, tiled=True)[0]
    stream_sum = stream_in + summed
    stream = stream_sum.astype(jnp.bfloat16)[None, None]
    normed = rms_scale(stream_sum, gain_out).astype(jnp.bfloat16)[None, None]
    return (stream, normed)


def swap_pair(x):
    return lax.ppermute(x, "dp", [(0, 1), (1, 0)])


def halves_swapped(x):
    half = x.shape[0] // 2
    return jnp.concatenate([x[half:], x[:half]], axis=0)


def in_axis_order(first, mine, peer, axis):
    return jnp.where(
        first, jnp.concatenate([mine, peer], axis=axis), jnp.concatenate([peer, mine], axis=axis)
    )


def shards_pair(
    attention,
    residual,
    out_proj,
    gain_in,
    router,
    expert_ids,
    live_rows,
    expert_gate,
    expert_up,
    expert_down,
    shared_gate,
    shared_up,
    shared_down,
    gain_out,
):
    groups = 2
    experts = lax.axis_size("expert")
    me = lax.axis_index("dp")
    first = me == 0
    row_count = attention.shape[2]
    top_count = expert_ids.shape[3]
    capacity = max(2, (2 * row_count * top_count + experts - 1) // experts)
    gate_local = expert_gate[0]
    up_local = expert_up[0]
    down_local = expert_down[0]
    column_width = down_local.shape[1]
    rows_all = groups * row_count

    attention_mine = attention[0, 0]
    residual_mine = residual[0, 0]
    attention_peer = swap_pair(attention_mine)
    residual_all = jnp.concatenate([residual_mine, swap_pair(residual_mine)], axis=0)
    product_mine = jnp.dot(attention_mine, out_proj, preferred_element_type=jnp.float32).astype(
        jnp.bfloat16
    )
    from_peer_for_peer = swap_pair(product_mine)
    product_peer = jnp.dot(attention_peer, out_proj, preferred_element_type=jnp.float32).astype(
        jnp.bfloat16
    )
    from_peer_for_mine = swap_pair(product_peer)
    projected = jnp.concatenate(
        [
            in_axis_order(first, product_mine, from_peer_for_mine, 1),
            in_axis_order(first, product_peer, from_peer_for_peer, 1),
        ],
        axis=0,
    )
    stream_all = residual_all.astype(jnp.float32) + projected.astype(jnp.float32)
    column = rms_scale(stream_all, gain_in).astype(jnp.bfloat16)
    stream_in = stream_all[:row_count]
    logit_part = jnp.dot(column, router, preferred_element_type=jnp.float32)
    logits = in_axis_order(first, logit_part, halves_swapped(swap_pair(logit_part)), 1)

    ids = expert_ids[0]
    ids_local = jnp.where(first, ids, ids[::-1])
    counts = live_rows[:, 0]
    counts_local = jnp.where(first, counts, counts[::-1])
    group_of_block = jnp.where(first, jnp.arange(groups), jnp.arange(groups)[::-1]).astype(jnp.int32)

    flat_experts = ids_local.reshape(rows_all, top_count)
    picked = jnp.take_along_axis(logits, flat_experts, axis=1)
    probabilities = jax.nn.softmax(picked, axis=1)
    row_live = (jnp.arange(row_count, dtype=jnp.int32)[None, :] < counts_local[:, None]).reshape(
        rows_all
    )
    slot_live = jnp.broadcast_to(row_live[:, None], (rows_all, top_count))
    weights = probabilities.astype(jnp.bfloat16) * slot_live.astype(jnp.bfloat16)
    block_experts = flat_experts.reshape(groups, row_count * top_count)
    block_live = slot_live.reshape(groups, row_count * top_count)
    onehot = (
        (block_experts[:, :, None] == jnp.arange(experts, dtype=jnp.int32)) & block_live[:, :, None]
    ).astype(jnp.int32)
    before = jnp.cumsum(onehot, axis=1) - onehot
    position = jnp.sum(before * onehot, axis=2)
    slot_total = experts * groups * capacity
    offsets = group_of_block[:, None] * capacity
    target = jnp.where(
        block_live, block_experts * (groups * capacity) + offsets + position, slot_total
    ).reshape(rows_all, top_count)
    slot_hit = target[:, :, None] == jnp.arange(slot_total, dtype=jnp.int32)[None, None, :]
    fill = jnp.any(slot_hit, axis=1).astype(jnp.bfloat16)
    outgoing = lax.dot_general(
        fill, column, (((0,), (0,)), ((), ())), preferred_element_type=jnp.float32
    ).astype(jnp.bfloat16).reshape(experts, groups * capacity, column.shape[1])
    slot_rows = lax.all_to_all(outgoing, "expert", split_axis=0, concat_axis=0, tiled=True)
    flattened = slot_rows.reshape(-1, slot_rows.shape[-1])
    gate_value = by_rows(flattened, gate_local)
    up_value = by_rows(flattened, up_local)
    hidden = (jax.nn.silu(gate_value) * up_value).astype(jnp.bfloat16)
    hidden_peer = swap_pair(hidden)
    shared_gate_value = by_rows(column, shared_gate)
    shared_up_value = by_rows(column, shared_up)
    shared_hidden = (jax.nn.silu(shared_gate_value) * shared_up_value).astype(jnp.bfloat16)
    shared_peer = halves_swapped(swap_pair(shared_hidden))

    unit_count = hidden.shape[1]
    down_blocks = down_local.reshape(groups, unit_count, column_width)
    shared_blocks = shared_down.reshape(groups, unit_count, column_width)
    down_mine = lax.dynamic_index_in_dim(down_blocks, me, 0, keepdims=False)
    down_peer = lax.dynamic_index_in_dim(down_blocks, 1 - me, 0, keepdims=False)
    shared_mine = lax.dynamic_index_in_dim(shared_blocks, me, 0, keepdims=False)
    shared_other = lax.dynamic_index_in_dim(shared_blocks, 1 - me, 0, keepdims=False)
    routed_total = jnp.dot(hidden, down_mine, preferred_element_type=jnp.float32) + jnp.dot(
        hidden_peer, down_peer, preferred_element_type=jnp.float32
    )
    shared = jnp.dot(shared_hidden, shared_mine, preferred_element_type=jnp.float32) + jnp.dot(
        shared_peer, shared_other, preferred_element_type=jnp.float32
    )
    expert_out = routed_total.astype(jnp.bfloat16).reshape(experts, groups * capacity, column_width)
    returned = lax.all_to_all(
        expert_out, "expert", split_axis=0, concat_axis=0, tiled=True
    ).reshape(slot_total, column_width)
    combine = jnp.sum(
        jnp.where(slot_hit, weights[:, :, None], jnp.zeros((), jnp.bfloat16)), axis=1
    ).astype(jnp.bfloat16)
    routed_peer = jnp.dot(combine[row_count:], returned, preferred_element_type=jnp.float32)
    combined_peer = jnp.where(row_live[row_count:, None], routed_peer + shared[row_count:], 0.0)
    from_peer = swap_pair(combined_peer)
    routed_mine = jnp.dot(combine[:row_count], returned, preferred_element_type=jnp.float32)
    combined_mine = jnp.where(row_live[:row_count, None], routed_mine + shared[:row_count], 0.0)
    summed = in_axis_order(first, combined_mine, from_peer, 1)
    stream_sum = stream_in + summed
    stream = stream_sum.astype(jnp.bfloat16)[None, None]
    normed = rms_scale(stream_sum, gain_out).astype(jnp.bfloat16)[None, None]
    return (stream, normed)


def shards(*args):
    if lax.axis_size("dp") == 2:
        return shards_pair(*args)
    return shards_general(*args)


def solution(mesh):
    placed = (
        P("expert", "dp", None, None),
        P("expert", "dp", None, None),
        P(None, "dp"),
        P(),
        P(None, "dp"),
        P("expert", None, None, None),
        P(None, "expert"),
        P("expert", "dp", None),
        P("expert", "dp", None),
        P("expert", None, "dp"),
        P("dp", None),
        P("dp", None),
        P(None, "dp"),
        P(),
    )
    return jax.shard_map(
        shards,
        mesh=mesh,
        in_specs=placed,
        out_specs=(P("expert", "dp", None, None), P("expert", "dp", None, None)),
        check_vma=False,
    )
```

```python
import jax
import jax.numpy as jnp
from jax import lax
from jax.experimental import pallas as pl
from jax.experimental.pallas import tpu as pltpu
from jax.sharding import PartitionSpec as P


def rms_scale(features, scale_gain):
    return (
        features
        * lax.rsqrt(jnp.mean(features * features, axis=-1, keepdims=True) + 1e-06)
        * scale_gain
    )


def by_rows(left, weight_rows):
    return lax.dot_general(
        left, weight_rows, (((1,), (1,)), ((), ())), preferred_element_type=jnp.float32
    )


def fill_slots(features, targets, slot_total, top_count):
    entries = jnp.arange(targets.shape[0], dtype=jnp.int32)
    source = jnp.full((slot_total,), -1, jnp.int32).at[targets].set(entries, mode="drop")
    chosen = jnp.take(features, jnp.maximum(source, 0) // top_count, axis=0)
    return jnp.where((source >= 0)[:, None], chosen, jnp.zeros_like(chosen))


def shards_general(
    attention,
    residual,
    out_proj,
    gain_in,
    router,
    expert_ids,
    live_rows,
    expert_gate,
    expert_up,
    expert_down,
    shared_gate,
    shared_up,
    shared_down,
    gain_out,
):
    groups = lax.axis_size("dp")
    experts = lax.axis_size("expert")
    row_count = attention.shape[2]
    feature_width = residual.shape[3]
    top_count = expert_ids.shape[3]
    capacity = max(2, (2 * row_count * top_count + experts - 1) // experts)
    gate_local = expert_gate[0]
    up_local = expert_up[0]
    down_local = expert_down[0]
    column_width = down_local.shape[1]
    pieces = lax.all_gather(attention, "dp", axis=1, tiled=True)
    flattened = pieces.reshape(-1, pieces.shape[-1])
    product = jnp.dot(flattened, out_proj, preferred_element_type=jnp.float32).astype(jnp.bfloat16)
    columns = product.reshape(pieces.shape[:-1] + (out_proj.shape[1],))
    projected = lax.all_to_all(columns, "dp", split_axis=1, concat_axis=3, tiled=True)[0, 0]
    stream_in = residual[0, 0].astype(jnp.float32) + projected.astype(jnp.float32)
    normal_rows = rms_scale(stream_in, gain_in).astype(jnp.bfloat16)
    column = lax.all_gather(normal_rows[None], "dp", axis=0, tiled=True).reshape(
        groups * row_count, feature_width
    )
    logit_part = jnp.dot(column, router, preferred_element_type=jnp.float32)
    logits = lax.all_gather(logit_part, "dp", axis=1, tiled=True)
    flat_experts = expert_ids[0].reshape(groups * row_count, top_count)
    picked = jnp.take_along_axis(logits, flat_experts, axis=1)
    probabilities = jax.nn.softmax(picked, axis=1)
    row_live = (jnp.arange(row_count, dtype=jnp.int32)[None, :] < live_rows[:, 0][:, None]).reshape(
        groups * row_count
    )
    slot_live = jnp.broadcast_to(row_live[:, None], (groups * row_count, top_count))
    weights = probabilities.astype(jnp.bfloat16) * slot_live.astype(jnp.bfloat16)
    block_experts = flat_experts.reshape(groups, row_count * top_count)
    block_live = slot_live.reshape(groups, row_count * top_count)
    onehot = (
        (block_experts[:, :, None] == jnp.arange(experts, dtype=jnp.int32)) & block_live[:, :, None]
    ).astype(jnp.int32)
    before = jnp.cumsum(onehot, axis=1) - onehot
    position = jnp.sum(before * onehot, axis=2)
    slot_total = experts * groups * capacity
    offsets = jnp.arange(groups, dtype=jnp.int32)[:, None] * capacity
    target = jnp.where(
        block_live, block_experts * (groups * capacity) + offsets + position, slot_total
    ).reshape(-1)
    outgoing = fill_slots(column, target, slot_total, top_count).reshape(
        experts, groups * capacity, feature_width
    )
    slot_rows = lax.all_to_all(outgoing, "expert", split_axis=0, concat_axis=0, tiled=True)
    flattened = slot_rows.reshape(-1, slot_rows.shape[-1])
    gate_value = by_rows(flattened, gate_local)
    up_value = by_rows(flattened, up_local)
    hidden = (jax.nn.silu(gate_value) * up_value).astype(jnp.bfloat16)
    routed_hidden = hidden.reshape(slot_rows.shape[:-1] + (gate_local.shape[0],))
    shared_gate_value = by_rows(column, shared_gate)
    shared_up_value = by_rows(column, shared_up)
    shared_hidden = (jax.nn.silu(shared_gate_value) * shared_up_value).astype(jnp.bfloat16)[None]
    routed_piece = lax.all_gather(routed_hidden, "dp", axis=2, tiled=True)
    shared_piece = lax.all_gather(shared_hidden, "dp", axis=2, tiled=True)
    count = routed_piece.shape[2]
    routed_total = jnp.dot(
        routed_piece.reshape(-1, count), down_local, preferred_element_type=jnp.float32
    )
    shared_total = jnp.dot(
        shared_piece.reshape(-1, shared_piece.shape[2]),
        shared_down,
        preferred_element_type=jnp.float32,
    )
    routed_total, shared = (routed_total, shared_total)
    expert_out = routed_total.astype(jnp.bfloat16).reshape(experts, groups * capacity, column_width)
    returned = lax.all_to_all(
        expert_out, "expert", split_axis=0, concat_axis=0, tiled=True
    ).reshape(slot_total, column_width)
    gathered = jnp.take(returned, jnp.minimum(target, slot_total - 1), axis=0).reshape(
        groups * row_count, top_count, column_width
    )
    routed = jnp.einsum("nk,nkd->nd", weights, gathered, preferred_element_type=jnp.float32)
    combined = jnp.where(row_live[:, None], routed + shared, 0.0).reshape(
        groups, row_count, column_width
    )
    summed = lax.all_to_all(combined, "dp", split_axis=0, concat_axis=2, tiled=True)[0]
    stream_sum = stream_in + summed
    stream = stream_sum.astype(jnp.bfloat16)[None, None]
    normed = rms_scale(stream_sum, gain_out).astype(jnp.bfloat16)[None, None]
    return (stream, normed)


def gate_up_kernel(rows_ref, gate_ref, up_ref, hidden_ref):
    rows = rows_ref[...]
    contract = (((1,), (1,)), ((), ()))
    gate_value = lax.dot_general(gate_ref[...], rows, contract, preferred_element_type=jnp.float32)
    up_value = lax.dot_general(up_ref[...], rows, contract, preferred_element_type=jnp.float32)
    silu = gate_value / (1.0 + jnp.exp(-gate_value))
    hidden_ref[...] = (silu * up_value).astype(hidden_ref.dtype)


def gate_up_transposed(rows, gate_weight, up_weight):
    count, width = rows.shape
    units = gate_weight.shape[0]
    tile = units // 4 if units % 64 == 0 else units
    return pl.pallas_call(
        gate_up_kernel,
        out_shape=jax.ShapeDtypeStruct((units, count), jnp.bfloat16),
        grid=(units // tile,),
        in_specs=[
            pl.BlockSpec((count, width), lambda i: (0, 0)),
            pl.BlockSpec((tile, width), lambda i: (i, 0)),
            pl.BlockSpec((tile, width), lambda i: (i, 0)),
        ],
        out_specs=pl.BlockSpec((tile, count), lambda i: (i, 0)),
        compiler_params=pltpu.CompilerParams(vmem_limit_bytes=48 * 1024 * 1024),
        cost_estimate=pl.CostEstimate(
            flops=4 * count * width * units,
            transcendentals=count * units,
            bytes_accessed=2 * (count * width + 2 * units * width + count * units),
        ),
    )(rows, gate_weight, up_weight)


def swap_pair(x):
    return lax.ppermute(x, "dp", [(0, 1), (1, 0)])


def halves_swapped(x):
    half = x.shape[0] // 2
    return jnp.concatenate([x[half:], x[:half]], axis=0)


def in_axis_order(first, mine, peer, axis):
    return jnp.where(
        first, jnp.concatenate([mine, peer], axis=axis), jnp.concatenate([peer, mine], axis=axis)
    )


def shards_pair(
    attention,
    residual,
    out_proj,
    gain_in,
    router,
    expert_ids,
    live_rows,
    expert_gate,
    expert_up,
    expert_down,
    shared_gate,
    shared_up,
    shared_down,
    gain_out,
):
    groups = 2
    experts = lax.axis_size("expert")
    me = lax.axis_index("dp")
    first = me == 0
    row_count = attention.shape[2]
    top_count = expert_ids.shape[3]
    capacity = max(2, (2 * row_count * top_count + experts - 1) // experts)
    gate_local = expert_gate[0]
    up_local = expert_up[0]
    down_local = expert_down[0]
    column_width = down_local.shape[1]
    rows_all = groups * row_count

    attention_mine = attention[0, 0]
    residual_mine = residual[0, 0]
    pieces = jnp.concatenate([attention_mine, swap_pair(attention_mine)], axis=0)
    residual_all = jnp.concatenate([residual_mine, swap_pair(residual_mine)], axis=0)
    product = jnp.dot(pieces, out_proj, preferred_element_type=jnp.float32).astype(jnp.bfloat16)
    projected = in_axis_order(first, product, halves_swapped(swap_pair(product)), 1)
    stream_all = residual_all.astype(jnp.float32) + projected.astype(jnp.float32)
    column = rms_scale(stream_all, gain_in).astype(jnp.bfloat16)
    stream_in = stream_all[:row_count]
    logit_part = jnp.dot(column, router, preferred_element_type=jnp.float32)
    logits = in_axis_order(first, logit_part, halves_swapped(swap_pair(logit_part)), 1)

    ids = expert_ids[0]
    ids_local = jnp.where(first, ids, ids[::-1])
    counts = live_rows[:, 0]
    counts_local = jnp.where(first, counts, counts[::-1])
    group_of_block = jnp.where(first, jnp.arange(groups), jnp.arange(groups)[::-1]).astype(jnp.int32)

    flat_experts = ids_local.reshape(rows_all, top_count)
    picked = jnp.take_along_axis(logits, flat_experts, axis=1)
    probabilities = jax.nn.softmax(picked, axis=1)
    row_live = (jnp.arange(row_count, dtype=jnp.int32)[None, :] < counts_local[:, None]).reshape(
        rows_all
    )
    slot_live = jnp.broadcast_to(row_live[:, None], (rows_all, top_count))
    weights = probabilities.astype(jnp.bfloat16) * slot_live.astype(jnp.bfloat16)
    block_experts = flat_experts.reshape(groups, row_count * top_count)
    block_live = slot_live.reshape(groups, row_count * top_count)
    onehot = (
        (block_experts[:, :, None] == jnp.arange(experts, dtype=jnp.int32)) & block_live[:, :, None]
    ).astype(jnp.int32)
    before = jnp.cumsum(onehot, axis=1) - onehot
    position = jnp.sum(before * onehot, axis=2)
    slot_total = experts * groups * capacity
    offsets = group_of_block[:, None] * capacity
    target = jnp.where(
        block_live, block_experts * (groups * capacity) + offsets + position, slot_total
    ).reshape(rows_all, top_count)
    slot_hit = target[:, :, None] == jnp.arange(slot_total, dtype=jnp.int32)[None, None, :]
    fill = jnp.any(slot_hit, axis=1).astype(jnp.bfloat16)
    outgoing = lax.dot_general(
        fill, column, (((0,), (0,)), ((), ())), preferred_element_type=jnp.float32
    ).astype(jnp.bfloat16).reshape(experts, groups * capacity, column.shape[1])
    slot_rows = lax.all_to_all(outgoing, "expert", split_axis=0, concat_axis=0, tiled=True)
    flattened = slot_rows.reshape(-1, slot_rows.shape[-1])
    hidden_t = gate_up_transposed(flattened, gate_local, up_local)
    hidden_peer_t = swap_pair(hidden_t)
    shared_gate_value = by_rows(column, shared_gate)
    shared_up_value = by_rows(column, shared_up)
    shared_hidden = (jax.nn.silu(shared_gate_value) * shared_up_value).astype(jnp.bfloat16)
    shared_peer = halves_swapped(swap_pair(shared_hidden))

    unit_count = hidden_t.shape[0]
    down_blocks = down_local.reshape(groups, unit_count, column_width)
    shared_blocks = shared_down.reshape(groups, unit_count, column_width)
    down_mine = lax.dynamic_index_in_dim(down_blocks, me, 0, keepdims=False)
    down_peer = lax.dynamic_index_in_dim(down_blocks, 1 - me, 0, keepdims=False)
    shared_mine = lax.dynamic_index_in_dim(shared_blocks, me, 0, keepdims=False)
    shared_other = lax.dynamic_index_in_dim(shared_blocks, 1 - me, 0, keepdims=False)
    by_units = (((0,), (0,)), ((), ()))
    routed_total = lax.dot_general(
        hidden_t, down_mine, by_units, preferred_element_type=jnp.float32
    ) + lax.dot_general(hidden_peer_t, down_peer, by_units, preferred_element_type=jnp.float32)
    shared = jnp.dot(shared_hidden, shared_mine, preferred_element_type=jnp.float32) + jnp.dot(
        shared_peer, shared_other, preferred_element_type=jnp.float32
    )
    expert_out = routed_total.astype(jnp.bfloat16).reshape(experts, groups * capacity, column_width)
    returned = lax.all_to_all(
        expert_out, "expert", split_axis=0, concat_axis=0, tiled=True
    ).reshape(slot_total, column_width)
    combine = jnp.sum(
        jnp.where(slot_hit, weights[:, :, None], jnp.zeros((), jnp.bfloat16)), axis=1
    ).astype(jnp.bfloat16)
    routed = jnp.dot(combine, returned, preferred_element_type=jnp.float32)
    combined = jnp.where(row_live[:, None], routed + shared, 0.0)
    summed = in_axis_order(first, combined[:row_count], swap_pair(combined[row_count:]), 1)
    stream_sum = stream_in + summed
    stream = stream_sum.astype(jnp.bfloat16)[None, None]
    normed = rms_scale(stream_sum, gain_out).astype(jnp.bfloat16)[None, None]
    return (stream, normed)


def shards(*args):
    if lax.axis_size("dp") == 2:
        return shards_pair(*args)
    return shards_general(*args)


def solution(mesh):
    placed = (
        P("expert", "dp", None, None),
        P("expert", "dp", None, None),
        P(None, "dp"),
        P(),
        P(None, "dp"),
        P("expert", None, None, None),
        P(None, "expert"),
        P("expert", "dp", None),
        P("expert", "dp", None),
        P("expert", None, "dp"),
        P("dp", None),
        P("dp", None),
        P(None, "dp"),
        P(),
    )
    return jax.shard_map(
        shards,
        mesh=mesh,
        in_specs=placed,
        out_specs=(P("expert", "dp", None, None), P("expert", "dp", None, None)),
        check_vma=False,
    )
```

```python
import jax
import jax.numpy as jnp
from jax import lax
from jax.sharding import PartitionSpec as P


def rms_scale(features, scale_gain):
    return (
        features
        * lax.rsqrt(jnp.mean(features * features, axis=-1, keepdims=True) + 1e-06)
        * scale_gain
    )


def by_rows(left, weight_rows):
    return lax.dot_general(
        left, weight_rows, (((1,), (1,)), ((), ())), preferred_element_type=jnp.float32
    )


def fill_slots(features, targets, slot_total, top_count):
    entries = jnp.arange(targets.shape[0], dtype=jnp.int32)
    source = jnp.full((slot_total,), -1, jnp.int32).at[targets].set(entries, mode="drop")
    chosen = jnp.take(features, jnp.maximum(source, 0) // top_count, axis=0)
    return jnp.where((source >= 0)[:, None], chosen, jnp.zeros_like(chosen))


def shards_general(
    attention,
    residual,
    out_proj,
    gain_in,
    router,
    expert_ids,
    live_rows,
    expert_gate,
    expert_up,
    expert_down,
    shared_gate,
    shared_up,
    shared_down,
    gain_out,
):
    groups = lax.axis_size("dp")
    experts = lax.axis_size("expert")
    row_count = attention.shape[2]
    feature_width = residual.shape[3]
    top_count = expert_ids.shape[3]
    capacity = max(2, (2 * row_count * top_count + experts - 1) // experts)
    gate_local = expert_gate[0]
    up_local = expert_up[0]
    down_local = expert_down[0]
    column_width = down_local.shape[1]
    pieces = lax.all_gather(attention, "dp", axis=1, tiled=True)
    flattened = pieces.reshape(-1, pieces.shape[-1])
    product = jnp.dot(flattened, out_proj, preferred_element_type=jnp.float32).astype(jnp.bfloat16)
    columns = product.reshape(pieces.shape[:-1] + (out_proj.shape[1],))
    projected = lax.all_to_all(columns, "dp", split_axis=1, concat_axis=3, tiled=True)[0, 0]
    stream_in = residual[0, 0].astype(jnp.float32) + projected.astype(jnp.float32)
    normal_rows = rms_scale(stream_in, gain_in).astype(jnp.bfloat16)
    column = lax.all_gather(normal_rows[None], "dp", axis=0, tiled=True).reshape(
        groups * row_count, feature_width
    )
    logit_part = jnp.dot(column, router, preferred_element_type=jnp.float32)
    logits = lax.all_gather(logit_part, "dp", axis=1, tiled=True)
    flat_experts = expert_ids[0].reshape(groups * row_count, top_count)
    picked = jnp.take_along_axis(logits, flat_experts, axis=1)
    probabilities = jax.nn.softmax(picked, axis=1)
    row_live = (jnp.arange(row_count, dtype=jnp.int32)[None, :] < live_rows[:, 0][:, None]).reshape(
        groups * row_count
    )
    slot_live = jnp.broadcast_to(row_live[:, None], (groups * row_count, top_count))
    weights = probabilities.astype(jnp.bfloat16) * slot_live.astype(jnp.bfloat16)
    block_experts = flat_experts.reshape(groups, row_count * top_count)
    block_live = slot_live.reshape(groups, row_count * top_count)
    onehot = (
        (block_experts[:, :, None] == jnp.arange(experts, dtype=jnp.int32)) & block_live[:, :, None]
    ).astype(jnp.int32)
    before = jnp.cumsum(onehot, axis=1) - onehot
    position = jnp.sum(before * onehot, axis=2)
    slot_total = experts * groups * capacity
    offsets = jnp.arange(groups, dtype=jnp.int32)[:, None] * capacity
    target = jnp.where(
        block_live, block_experts * (groups * capacity) + offsets + position, slot_total
    ).reshape(-1)
    outgoing = fill_slots(column, target, slot_total, top_count).reshape(
        experts, groups * capacity, feature_width
    )
    slot_rows = lax.all_to_all(outgoing, "expert", split_axis=0, concat_axis=0, tiled=True)
    flattened = slot_rows.reshape(-1, slot_rows.shape[-1])
    gate_value = by_rows(flattened, gate_local)
    up_value = by_rows(flattened, up_local)
    hidden = (jax.nn.silu(gate_value) * up_value).astype(jnp.bfloat16)
    routed_hidden = hidden.reshape(slot_rows.shape[:-1] + (gate_local.shape[0],))
    shared_gate_value = by_rows(column, shared_gate)
    shared_up_value = by_rows(column, shared_up)
    shared_hidden = (jax.nn.silu(shared_gate_value) * shared_up_value).astype(jnp.bfloat16)[None]
    routed_piece = lax.all_gather(routed_hidden, "dp", axis=2, tiled=True)
    shared_piece = lax.all_gather(shared_hidden, "dp", axis=2, tiled=True)
    count = routed_piece.shape[2]
    routed_total = jnp.dot(
        routed_piece.reshape(-1, count), down_local, preferred_element_type=jnp.float32
    )
    shared_total = jnp.dot(
        shared_piece.reshape(-1, shared_piece.shape[2]),
        shared_down,
        preferred_element_type=jnp.float32,
    )
    routed_total, shared = (routed_total, shared_total)
    expert_out = routed_total.astype(jnp.bfloat16).reshape(experts, groups * capacity, column_width)
    returned = lax.all_to_all(
        expert_out, "expert", split_axis=0, concat_axis=0, tiled=True
    ).reshape(slot_total, column_width)
    gathered = jnp.take(returned, jnp.minimum(target, slot_total - 1), axis=0).reshape(
        groups * row_count, top_count, column_width
    )
    routed = jnp.einsum("nk,nkd->nd", weights, gathered, preferred_element_type=jnp.float32)
    combined = jnp.where(row_live[:, None], routed + shared, 0.0).reshape(
        groups, row_count, column_width
    )
    summed = lax.all_to_all(combined, "dp", split_axis=0, concat_axis=2, tiled=True)[0]
    stream_sum = stream_in + summed
    stream = stream_sum.astype(jnp.bfloat16)[None, None]
    normed = rms_scale(stream_sum, gain_out).astype(jnp.bfloat16)[None, None]
    return (stream, normed)


def swap_pair(x):
    return lax.ppermute(x, "dp", [(0, 1), (1, 0)])


def halves_swapped(x):
    half = x.shape[0] // 2
    return jnp.concatenate([x[half:], x[:half]], axis=0)


def in_axis_order(first, mine, peer, axis):
    return jnp.where(
        first, jnp.concatenate([mine, peer], axis=axis), jnp.concatenate([peer, mine], axis=axis)
    )


def shards_pair(
    attention,
    residual,
    out_proj,
    gain_in,
    router,
    expert_ids,
    live_rows,
    expert_gate,
    expert_up,
    expert_down,
    shared_gate,
    shared_up,
    shared_down,
    gain_out,
):
    groups = 2
    experts = lax.axis_size("expert")
    me = lax.axis_index("dp")
    first = me == 0
    row_count = attention.shape[2]
    top_count = expert_ids.shape[3]
    capacity = max(2, (2 * row_count * top_count + experts - 1) // experts)
    gate_local = expert_gate[0]
    up_local = expert_up[0]
    down_local = expert_down[0]
    column_width = down_local.shape[1]
    rows_all = groups * row_count

    attention_mine = attention[0, 0]
    residual_mine = residual[0, 0]
    pieces = jnp.concatenate([attention_mine, swap_pair(attention_mine)], axis=0)
    residual_all = jnp.concatenate([residual_mine, swap_pair(residual_mine)], axis=0)
    product = jnp.dot(pieces, out_proj, preferred_element_type=jnp.float32).astype(jnp.bfloat16)
    projected = in_axis_order(first, product, halves_swapped(swap_pair(product)), 1)
    stream_all = residual_all.astype(jnp.float32) + projected.astype(jnp.float32)
    column = rms_scale(stream_all, gain_in).astype(jnp.bfloat16)
    stream_in = stream_all[:row_count]
    logit_part = jnp.dot(column, router, preferred_element_type=jnp.float32)
    logits = in_axis_order(first, logit_part, halves_swapped(swap_pair(logit_part)), 1)

    ids = expert_ids[0]
    ids_local = jnp.where(first, ids, ids[::-1])
    counts = live_rows[:, 0]
    counts_local = jnp.where(first, counts, counts[::-1])
    group_of_block = jnp.where(first, jnp.arange(groups), jnp.arange(groups)[::-1]).astype(jnp.int32)

    flat_experts = ids_local.reshape(rows_all, top_count)
    picked = jnp.take_along_axis(logits, flat_experts, axis=1)
    probabilities = jax.nn.softmax(picked, axis=1)
    row_live = (jnp.arange(row_count, dtype=jnp.int32)[None, :] < counts_local[:, None]).reshape(
        rows_all
    )
    slot_live = jnp.broadcast_to(row_live[:, None], (rows_all, top_count))
    weights = probabilities.astype(jnp.bfloat16) * slot_live.astype(jnp.bfloat16)
    block_experts = flat_experts.reshape(groups, row_count * top_count)
    block_live = slot_live.reshape(groups, row_count * top_count)
    onehot = (
        (block_experts[:, :, None] == jnp.arange(experts, dtype=jnp.int32)) & block_live[:, :, None]
    ).astype(jnp.int32)
    before = jnp.cumsum(onehot, axis=1) - onehot
    position = jnp.sum(before * onehot, axis=2)
    slot_total = experts * groups * capacity
    offsets = group_of_block[:, None] * capacity
    target = jnp.where(
        block_live, block_experts * (groups * capacity) + offsets + position, slot_total
    ).reshape(rows_all, top_count)
    slot_hit = target[:, :, None] == jnp.arange(slot_total, dtype=jnp.int32)[None, None, :]
    fill = jnp.any(slot_hit, axis=1).astype(jnp.bfloat16)
    outgoing = lax.dot_general(
        fill, column, (((0,), (0,)), ((), ())), preferred_element_type=jnp.float32
    ).astype(jnp.bfloat16).reshape(experts, groups * capacity, column.shape[1])
    slot_rows = lax.all_to_all(outgoing, "expert", split_axis=0, concat_axis=0, tiled=True)
    flattened = slot_rows.reshape(-1, slot_rows.shape[-1])
    gate_value = by_rows(flattened, gate_local)
    up_value = by_rows(flattened, up_local)
    hidden = (jax.nn.silu(gate_value) * up_value).astype(jnp.bfloat16)
    hidden_peer = swap_pair(hidden)
    shared_gate_value = by_rows(column, shared_gate)
    shared_up_value = by_rows(column, shared_up)
    shared_hidden = (jax.nn.silu(shared_gate_value) * shared_up_value).astype(jnp.bfloat16)
    shared_peer = halves_swapped(swap_pair(shared_hidden))

    unit_count = hidden.shape[1]
    down_blocks = down_local.reshape(groups, unit_count, column_width)
    shared_blocks = shared_down.reshape(groups, unit_count, column_width)
    down_mine = lax.dynamic_index_in_dim(down_blocks, me, 0, keepdims=False)
    down_peer = lax.dynamic_index_in_dim(down_blocks, 1 - me, 0, keepdims=False)
    shared_mine = lax.dynamic_index_in_dim(shared_blocks, me, 0, keepdims=False)
    shared_other = lax.dynamic_index_in_dim(shared_blocks, 1 - me, 0, keepdims=False)
    routed_total = jnp.dot(hidden, down_mine, preferred_element_type=jnp.float32) + jnp.dot(
        hidden_peer, down_peer, preferred_element_type=jnp.float32
    )
    shared = jnp.dot(shared_hidden, shared_mine, preferred_element_type=jnp.float32) + jnp.dot(
        shared_peer, shared_other, preferred_element_type=jnp.float32
    )
    expert_out = routed_total.astype(jnp.bfloat16).reshape(experts, groups * capacity, column_width)
    returned = lax.all_to_all(
        expert_out, "expert", split_axis=0, concat_axis=0, tiled=True
    ).reshape(slot_total, column_width)
    combine = jnp.sum(
        jnp.where(slot_hit, weights[:, :, None], jnp.zeros((), jnp.bfloat16)), axis=1
    ).astype(jnp.bfloat16)
    routed_peer = jnp.dot(combine[row_count:], returned, preferred_element_type=jnp.float32)
    combined_peer = jnp.where(row_live[row_count:, None], routed_peer + shared[row_count:], 0.0)
    from_peer = swap_pair(combined_peer)
    routed_mine = jnp.dot(combine[:row_count], returned, preferred_element_type=jnp.float32)
    combined_mine = jnp.where(row_live[:row_count, None], routed_mine + shared[:row_count], 0.0)
    summed = in_axis_order(first, combined_mine, from_peer, 1)
    stream_sum = stream_in + summed
    stream = stream_sum.astype(jnp.bfloat16)[None, None]
    normed = rms_scale(stream_sum, gain_out).astype(jnp.bfloat16)[None, None]
    return (stream, normed)


def shards(*args):
    if lax.axis_size("dp") == 2:
        return shards_pair(*args)
    return shards_general(*args)


def solution(mesh):
    placed = (
        P("expert", "dp", None, None),
        P("expert", "dp", None, None),
        P(None, "dp"),
        P(),
        P(None, "dp"),
        P("expert", None, None, None),
        P(None, "expert"),
        P("expert", "dp", None),
        P("expert", "dp", None),
        P("expert", None, "dp"),
        P("dp", None),
        P("dp", None),
        P(None, "dp"),
        P(),
    )
    return jax.shard_map(
        shards,
        mesh=mesh,
        in_specs=placed,
        out_specs=(P("expert", "dp", None, None), P("expert", "dp", None, None)),
        check_vma=False,
    )
```

```python
import jax
import jax.numpy as jnp
from jax import lax
from jax.sharding import PartitionSpec as P


def rms_scale(features, scale_gain):
    return (
        features
        * lax.rsqrt(jnp.mean(features * features, axis=-1, keepdims=True) + 1e-06)
        * scale_gain
    )


def by_rows(left, weight_rows):
    return lax.dot_general(
        left, weight_rows, (((1,), (1,)), ((), ())), preferred_element_type=jnp.float32
    )


def fill_slots(features, targets, slot_total, top_count):
    entries = jnp.arange(targets.shape[0], dtype=jnp.int32)
    source = jnp.full((slot_total,), -1, jnp.int32).at[targets].set(entries, mode="drop")
    chosen = jnp.take(features, jnp.maximum(source, 0) // top_count, axis=0)
    return jnp.where((source >= 0)[:, None], chosen, jnp.zeros_like(chosen))


def shards_general(
    attention,
    residual,
    out_proj,
    gain_in,
    router,
    expert_ids,
    live_rows,
    expert_gate,
    expert_up,
    expert_down,
    shared_gate,
    shared_up,
    shared_down,
    gain_out,
):
    groups = lax.axis_size("dp")
    experts = lax.axis_size("expert")
    row_count = attention.shape[2]
    feature_width = residual.shape[3]
    top_count = expert_ids.shape[3]
    capacity = max(2, (2 * row_count * top_count + experts - 1) // experts)
    gate_local = expert_gate[0]
    up_local = expert_up[0]
    down_local = expert_down[0]
    column_width = down_local.shape[1]
    pieces = lax.all_gather(attention, "dp", axis=1, tiled=True)
    flattened = pieces.reshape(-1, pieces.shape[-1])
    product = jnp.dot(flattened, out_proj, preferred_element_type=jnp.float32).astype(jnp.bfloat16)
    columns = product.reshape(pieces.shape[:-1] + (out_proj.shape[1],))
    projected = lax.all_to_all(columns, "dp", split_axis=1, concat_axis=3, tiled=True)[0, 0]
    stream_in = residual[0, 0].astype(jnp.float32) + projected.astype(jnp.float32)
    normal_rows = rms_scale(stream_in, gain_in).astype(jnp.bfloat16)
    column = lax.all_gather(normal_rows[None], "dp", axis=0, tiled=True).reshape(
        groups * row_count, feature_width
    )
    logit_part = jnp.dot(column, router, preferred_element_type=jnp.float32)
    logits = lax.all_gather(logit_part, "dp", axis=1, tiled=True)
    flat_experts = expert_ids[0].reshape(groups * row_count, top_count)
    picked = jnp.take_along_axis(logits, flat_experts, axis=1)
    probabilities = jax.nn.softmax(picked, axis=1)
    row_live = (jnp.arange(row_count, dtype=jnp.int32)[None, :] < live_rows[:, 0][:, None]).reshape(
        groups * row_count
    )
    slot_live = jnp.broadcast_to(row_live[:, None], (groups * row_count, top_count))
    weights = probabilities.astype(jnp.bfloat16) * slot_live.astype(jnp.bfloat16)
    block_experts = flat_experts.reshape(groups, row_count * top_count)
    block_live = slot_live.reshape(groups, row_count * top_count)
    onehot = (
        (block_experts[:, :, None] == jnp.arange(experts, dtype=jnp.int32)) & block_live[:, :, None]
    ).astype(jnp.int32)
    before = jnp.cumsum(onehot, axis=1) - onehot
    position = jnp.sum(before * onehot, axis=2)
    slot_total = experts * groups * capacity
    offsets = jnp.arange(groups, dtype=jnp.int32)[:, None] * capacity
    target = jnp.where(
        block_live, block_experts * (groups * capacity) + offsets + position, slot_total
    ).reshape(-1)
    outgoing = fill_slots(column, target, slot_total, top_count).reshape(
        experts, groups * capacity, feature_width
    )
    slot_rows = lax.all_to_all(outgoing, "expert", split_axis=0, concat_axis=0, tiled=True)
    flattened = slot_rows.reshape(-1, slot_rows.shape[-1])
    gate_value = by_rows(flattened, gate_local)
    up_value = by_rows(flattened, up_local)
    hidden = (jax.nn.silu(gate_value) * up_value).astype(jnp.bfloat16)
    routed_hidden = hidden.reshape(slot_rows.shape[:-1] + (gate_local.shape[0],))
    shared_gate_value = by_rows(column, shared_gate)
    shared_up_value = by_rows(column, shared_up)
    shared_hidden = (jax.nn.silu(shared_gate_value) * shared_up_value).astype(jnp.bfloat16)[None]
    routed_piece = lax.all_gather(routed_hidden, "dp", axis=2, tiled=True)
    shared_piece = lax.all_gather(shared_hidden, "dp", axis=2, tiled=True)
    count = routed_piece.shape[2]
    routed_total = jnp.dot(
        routed_piece.reshape(-1, count), down_local, preferred_element_type=jnp.float32
    )
    shared_total = jnp.dot(
        shared_piece.reshape(-1, shared_piece.shape[2]),
        shared_down,
        preferred_element_type=jnp.float32,
    )
    routed_total, shared = (routed_total, shared_total)
    expert_out = routed_total.astype(jnp.bfloat16).reshape(experts, groups * capacity, column_width)
    returned = lax.all_to_all(
        expert_out, "expert", split_axis=0, concat_axis=0, tiled=True
    ).reshape(slot_total, column_width)
    gathered = jnp.take(returned, jnp.minimum(target, slot_total - 1), axis=0).reshape(
        groups * row_count, top_count, column_width
    )
    routed = jnp.einsum("nk,nkd->nd", weights, gathered, preferred_element_type=jnp.float32)
    combined = jnp.where(row_live[:, None], routed + shared, 0.0).reshape(
        groups, row_count, column_width
    )
    summed = lax.all_to_all(combined, "dp", split_axis=0, concat_axis=2, tiled=True)[0]
    stream_sum = stream_in + summed
    stream = stream_sum.astype(jnp.bfloat16)[None, None]
    normed = rms_scale(stream_sum, gain_out).astype(jnp.bfloat16)[None, None]
    return (stream, normed)


def swap_pair(x):
    return lax.ppermute(x, "dp", [(0, 1), (1, 0)])


def halves_swapped(x):
    half = x.shape[0] // 2
    return jnp.concatenate([x[half:], x[:half]], axis=0)


def in_axis_order(first, mine, peer, axis):
    return jnp.where(
        first, jnp.concatenate([mine, peer], axis=axis), jnp.concatenate([peer, mine], axis=axis)
    )


def shards_pair(
    attention,
    residual,
    out_proj,
    gain_in,
    router,
    expert_ids,
    live_rows,
    expert_gate,
    expert_up,
    expert_down,
    shared_gate,
    shared_up,
    shared_down,
    gain_out,
):
    groups = 2
    experts = lax.axis_size("expert")
    me = lax.axis_index("dp")
    first = me == 0
    row_count = attention.shape[2]
    top_count = expert_ids.shape[3]
    capacity = max(2, (2 * row_count * top_count + experts - 1) // experts)
    gate_local = expert_gate[0]
    up_local = expert_up[0]
    down_local = expert_down[0]
    column_width = down_local.shape[1]
    rows_all = groups * row_count

    attention_mine = attention[0, 0]
    residual_mine = residual[0, 0]
    pieces = jnp.concatenate([attention_mine, swap_pair(attention_mine)], axis=0)
    residual_all = jnp.concatenate([residual_mine, swap_pair(residual_mine)], axis=0)
    product = jnp.dot(pieces, out_proj, preferred_element_type=jnp.float32).astype(jnp.bfloat16)
    projected = in_axis_order(first, product, halves_swapped(swap_pair(product)), 1)
    stream_all = residual_all.astype(jnp.float32) + projected.astype(jnp.float32)
    column = rms_scale(stream_all, gain_in).astype(jnp.bfloat16)
    stream_in = stream_all[:row_count]
    logit_part = jnp.dot(column, router, preferred_element_type=jnp.float32)
    logits = in_axis_order(first, logit_part, halves_swapped(swap_pair(logit_part)), 1)

    ids = expert_ids[0]
    ids_local = jnp.where(first, ids, ids[::-1])
    counts = live_rows[:, 0]
    counts_local = jnp.where(first, counts, counts[::-1])
    group_of_block = jnp.where(first, jnp.arange(groups), jnp.arange(groups)[::-1]).astype(jnp.int32)

    flat_experts = ids_local.reshape(rows_all, top_count)
    picked = jnp.take_along_axis(logits, flat_experts, axis=1)
    probabilities = jax.nn.softmax(picked, axis=1)
    row_live = (jnp.arange(row_count, dtype=jnp.int32)[None, :] < counts_local[:, None]).reshape(
        rows_all
    )
    slot_live = jnp.broadcast_to(row_live[:, None], (rows_all, top_count))
    weights = probabilities.astype(jnp.bfloat16) * slot_live.astype(jnp.bfloat16)
    block_experts = flat_experts.reshape(groups, row_count * top_count)
    block_live = slot_live.reshape(groups, row_count * top_count)
    onehot = (
        (block_experts[:, :, None] == jnp.arange(experts, dtype=jnp.int32)) & block_live[:, :, None]
    ).astype(jnp.int32)
    before = jnp.cumsum(onehot, axis=1) - onehot
    position = jnp.sum(before * onehot, axis=2)
    slot_total = experts * groups * capacity
    offsets = jnp.arange(groups, dtype=jnp.int32)[:, None] * capacity
    target = jnp.where(
        block_live, block_experts * (groups * capacity) + offsets + position, slot_total
    ).reshape(rows_all, top_count)
    slot_hit = target[:, :, None] == jnp.arange(slot_total, dtype=jnp.int32)[None, None, :]
    own_total = experts * capacity
    own_target = jnp.where(
        block_live[0], block_experts[0] * capacity + position[0], own_total
    ).reshape(row_count, top_count)
    own_hit = own_target[:, :, None] == jnp.arange(own_total, dtype=jnp.int32)[None, None, :]
    fill = jnp.any(own_hit, axis=1).astype(jnp.bfloat16)
    outgoing = lax.dot_general(
        fill, column[:row_count], (((0,), (0,)), ((), ())), preferred_element_type=jnp.float32
    ).astype(jnp.bfloat16).reshape(experts, capacity, column.shape[1])
    slot_own = lax.all_to_all(outgoing, "expert", split_axis=0, concat_axis=0, tiled=True)
    slot_own = slot_own.reshape(-1, slot_own.shape[-1])
    slot_other = swap_pair(slot_own)
    hidden_own = (jax.nn.silu(by_rows(slot_own, gate_local)) * by_rows(slot_own, up_local)).astype(
        jnp.bfloat16
    )
    hidden_own_peer = swap_pair(hidden_own)
    hidden_other = (
        jax.nn.silu(by_rows(slot_other, gate_local)) * by_rows(slot_other, up_local)
    ).astype(jnp.bfloat16)
    hidden_other_peer = swap_pair(hidden_other)
    shared_gate_value = by_rows(column, shared_gate)
    shared_up_value = by_rows(column, shared_up)
    shared_hidden = (jax.nn.silu(shared_gate_value) * shared_up_value).astype(jnp.bfloat16)
    shared_peer = halves_swapped(swap_pair(shared_hidden))

    unit_count = hidden_own.shape[1]
    down_blocks = down_local.reshape(groups, unit_count, column_width)
    shared_blocks = shared_down.reshape(groups, unit_count, column_width)
    down_mine = lax.dynamic_index_in_dim(down_blocks, me, 0, keepdims=False)
    down_peer = lax.dynamic_index_in_dim(down_blocks, 1 - me, 0, keepdims=False)
    shared_mine = lax.dynamic_index_in_dim(shared_blocks, me, 0, keepdims=False)
    shared_other = lax.dynamic_index_in_dim(shared_blocks, 1 - me, 0, keepdims=False)
    out_own = jnp.dot(hidden_own, down_mine, preferred_element_type=jnp.float32) + jnp.dot(
        hidden_other_peer, down_peer, preferred_element_type=jnp.float32
    )
    out_other = jnp.dot(hidden_other, down_mine, preferred_element_type=jnp.float32) + jnp.dot(
        hidden_own_peer, down_peer, preferred_element_type=jnp.float32
    )
    shared = jnp.dot(shared_hidden, shared_mine, preferred_element_type=jnp.float32) + jnp.dot(
        shared_peer, shared_other, preferred_element_type=jnp.float32
    )
    expert_out = jnp.concatenate(
        [
            out_own.astype(jnp.bfloat16).reshape(experts, capacity, column_width),
            out_other.astype(jnp.bfloat16).reshape(experts, capacity, column_width),
        ],
        axis=1,
    )
    returned = lax.all_to_all(
        expert_out, "expert", split_axis=0, concat_axis=0, tiled=True
    ).reshape(slot_total, column_width)
    combine = jnp.sum(
        jnp.where(slot_hit, weights[:, :, None], jnp.zeros((), jnp.bfloat16)), axis=1
    ).astype(jnp.bfloat16)
    routed = jnp.dot(combine, returned, preferred_element_type=jnp.float32)
    combined = jnp.where(row_live[:, None], routed + shared, 0.0)
    summed = in_axis_order(first, combined[:row_count], swap_pair(combined[row_count:]), 1)
    stream_sum = stream_in + summed
    stream = stream_sum.astype(jnp.bfloat16)[None, None]
    normed = rms_scale(stream_sum, gain_out).astype(jnp.bfloat16)[None, None]
    return (stream, normed)


def shards(*args):
    if lax.axis_size("dp") == 2:
        return shards_pair(*args)
    return shards_general(*args)


def solution(mesh):
    placed = (
        P("expert", "dp", None, None),
        P("expert", "dp", None, None),
        P(None, "dp"),
        P(),
        P(None, "dp"),
        P("expert", None, None, None),
        P(None, "expert"),
        P("expert", "dp", None),
        P("expert", "dp", None),
        P("expert", None, "dp"),
        P("dp", None),
        P("dp", None),
        P(None, "dp"),
        P(),
    )
    return jax.shard_map(
        shards,
        mesh=mesh,
        in_specs=placed,
        out_specs=(P("expert", "dp", None, None), P("expert", "dp", None, None)),
        check_vma=False,
    )
```

```python
import jax
import jax.numpy as jnp
from jax import lax
from jax.sharding import PartitionSpec as P


def rms_scale(features, scale_gain):
    return (
        features
        * lax.rsqrt(jnp.mean(features * features, axis=-1, keepdims=True) + 1e-06)
        * scale_gain
    )


def by_rows(left, weight_rows):
    return lax.dot_general(
        left, weight_rows, (((1,), (1,)), ((), ())), preferred_element_type=jnp.float32
    )


def fill_slots(features, targets, slot_total, top_count):
    entries = jnp.arange(targets.shape[0], dtype=jnp.int32)
    source = jnp.full((slot_total,), -1, jnp.int32).at[targets].set(entries, mode="drop")
    chosen = jnp.take(features, jnp.maximum(source, 0) // top_count, axis=0)
    return jnp.where((source >= 0)[:, None], chosen, jnp.zeros_like(chosen))


def shards_general(
    attention,
    residual,
    out_proj,
    gain_in,
    router,
    expert_ids,
    live_rows,
    expert_gate,
    expert_up,
    expert_down,
    shared_gate,
    shared_up,
    shared_down,
    gain_out,
):
    groups = lax.axis_size("dp")
    experts = lax.axis_size("expert")
    row_count = attention.shape[2]
    feature_width = residual.shape[3]
    top_count = expert_ids.shape[3]
    capacity = max(2, (2 * row_count * top_count + experts - 1) // experts)
    gate_local = expert_gate[0]
    up_local = expert_up[0]
    down_local = expert_down[0]
    column_width = down_local.shape[1]
    pieces = lax.all_gather(attention, "dp", axis=1, tiled=True)
    flattened = pieces.reshape(-1, pieces.shape[-1])
    product = jnp.dot(flattened, out_proj, preferred_element_type=jnp.float32).astype(jnp.bfloat16)
    columns = product.reshape(pieces.shape[:-1] + (out_proj.shape[1],))
    projected = lax.all_to_all(columns, "dp", split_axis=1, concat_axis=3, tiled=True)[0, 0]
    stream_in = residual[0, 0].astype(jnp.float32) + projected.astype(jnp.float32)
    normal_rows = rms_scale(stream_in, gain_in).astype(jnp.bfloat16)
    column = lax.all_gather(normal_rows[None], "dp", axis=0, tiled=True).reshape(
        groups * row_count, feature_width
    )
    logit_part = jnp.dot(column, router, preferred_element_type=jnp.float32)
    logits = lax.all_gather(logit_part, "dp", axis=1, tiled=True)
    flat_experts = expert_ids[0].reshape(groups * row_count, top_count)
    picked = jnp.take_along_axis(logits, flat_experts, axis=1)
    probabilities = jax.nn.softmax(picked, axis=1)
    row_live = (jnp.arange(row_count, dtype=jnp.int32)[None, :] < live_rows[:, 0][:, None]).reshape(
        groups * row_count
    )
    slot_live = jnp.broadcast_to(row_live[:, None], (groups * row_count, top_count))
    weights = probabilities.astype(jnp.bfloat16) * slot_live.astype(jnp.bfloat16)
    block_experts = flat_experts.reshape(groups, row_count * top_count)
    block_live = slot_live.reshape(groups, row_count * top_count)
    onehot = (
        (block_experts[:, :, None] == jnp.arange(experts, dtype=jnp.int32)) & block_live[:, :, None]
    ).astype(jnp.int32)
    before = jnp.cumsum(onehot, axis=1) - onehot
    position = jnp.sum(before * onehot, axis=2)
    slot_total = experts * groups * capacity
    offsets = jnp.arange(groups, dtype=jnp.int32)[:, None] * capacity
    target = jnp.where(
        block_live, block_experts * (groups * capacity) + offsets + position, slot_total
    ).reshape(-1)
    outgoing = fill_slots(column, target, slot_total, top_count).reshape(
        experts, groups * capacity, feature_width
    )
    slot_rows = lax.all_to_all(outgoing, "expert", split_axis=0, concat_axis=0, tiled=True)
    flattened = slot_rows.reshape(-1, slot_rows.shape[-1])
    gate_value = by_rows(flattened, gate_local)
    up_value = by_rows(flattened, up_local)
    hidden = (jax.nn.silu(gate_value) * up_value).astype(jnp.bfloat16)
    routed_hidden = hidden.reshape(slot_rows.shape[:-1] + (gate_local.shape[0],))
    shared_gate_value = by_rows(column, shared_gate)
    shared_up_value = by_rows(column, shared_up)
    shared_hidden = (jax.nn.silu(shared_gate_value) * shared_up_value).astype(jnp.bfloat16)[None]
    routed_piece = lax.all_gather(routed_hidden, "dp", axis=2, tiled=True)
    shared_piece = lax.all_gather(shared_hidden, "dp", axis=2, tiled=True)
    count = routed_piece.shape[2]
    routed_total = jnp.dot(
        routed_piece.reshape(-1, count), down_local, preferred_element_type=jnp.float32
    )
    shared_total = jnp.dot(
        shared_piece.reshape(-1, shared_piece.shape[2]),
        shared_down,
        preferred_element_type=jnp.float32,
    )
    routed_total, shared = (routed_total, shared_total)
    expert_out = routed_total.astype(jnp.bfloat16).reshape(experts, groups * capacity, column_width)
    returned = lax.all_to_all(
        expert_out, "expert", split_axis=0, concat_axis=0, tiled=True
    ).reshape(slot_total, column_width)
    gathered = jnp.take(returned, jnp.minimum(target, slot_total - 1), axis=0).reshape(
        groups * row_count, top_count, column_width
    )
    routed = jnp.einsum("nk,nkd->nd", weights, gathered, preferred_element_type=jnp.float32)
    combined = jnp.where(row_live[:, None], routed + shared, 0.0).reshape(
        groups, row_count, column_width
    )
    summed = lax.all_to_all(combined, "dp", split_axis=0, concat_axis=2, tiled=True)[0]
    stream_sum = stream_in + summed
    stream = stream_sum.astype(jnp.bfloat16)[None, None]
    normed = rms_scale(stream_sum, gain_out).astype(jnp.bfloat16)[None, None]
    return (stream, normed)


def swap_pair(x):
    return lax.ppermute(x, "dp", [(0, 1), (1, 0)])


def halves_swapped(x):
    half = x.shape[0] // 2
    return jnp.concatenate([x[half:], x[:half]], axis=0)


def in_axis_order(first, mine, peer, axis):
    return jnp.where(
        first, jnp.concatenate([mine, peer], axis=axis), jnp.concatenate([peer, mine], axis=axis)
    )


def shards_pair(
    attention,
    residual,
    out_proj,
    gain_in,
    router,
    expert_ids,
    live_rows,
    expert_gate,
    expert_up,
    expert_down,
    shared_gate,
    shared_up,
    shared_down,
    gain_out,
):
    groups = 2
    experts = lax.axis_size("expert")
    me = lax.axis_index("dp")
    first = me == 0
    row_count = attention.shape[2]
    top_count = expert_ids.shape[3]
    capacity = max(2, (2 * row_count * top_count + experts - 1) // experts)
    gate_local = expert_gate[0]
    up_local = expert_up[0]
    down_local = expert_down[0]
    column_width = down_local.shape[1]
    rows_all = groups * row_count

    attention_mine = attention[0, 0]
    residual_mine = residual[0, 0]
    pieces = jnp.concatenate([attention_mine, swap_pair(attention_mine)], axis=0)
    residual_all = jnp.concatenate([residual_mine, swap_pair(residual_mine)], axis=0)
    product = jnp.dot(pieces, out_proj, preferred_element_type=jnp.float32).astype(jnp.bfloat16)
    projected = in_axis_order(first, product, halves_swapped(swap_pair(product)), 1)
    stream_all = residual_all.astype(jnp.float32) + projected.astype(jnp.float32)
    column = rms_scale(stream_all, gain_in).astype(jnp.bfloat16)
    stream_in = stream_all[:row_count]
    logit_part = jnp.dot(column, router, preferred_element_type=jnp.float32)
    logits = in_axis_order(first, logit_part, halves_swapped(swap_pair(logit_part)), 1)

    ids = expert_ids[0]
    ids_local = jnp.where(first, ids, ids[::-1])
    counts = live_rows[:, 0]
    counts_local = jnp.where(first, counts, counts[::-1])
    group_of_block = jnp.where(first, jnp.arange(groups), jnp.arange(groups)[::-1]).astype(jnp.int32)

    flat_experts = ids_local.reshape(rows_all, top_count)
    picked = jnp.take_along_axis(logits, flat_experts, axis=1)
    probabilities = jax.nn.softmax(picked, axis=1)
    row_live = (jnp.arange(row_count, dtype=jnp.int32)[None, :] < counts_local[:, None]).reshape(
        rows_all
    )
    slot_live = jnp.broadcast_to(row_live[:, None], (rows_all, top_count))
    weights = probabilities.astype(jnp.bfloat16) * slot_live.astype(jnp.bfloat16)
    block_experts = flat_experts.reshape(groups, row_count * top_count)
    block_live = slot_live.reshape(groups, row_count * top_count)
    onehot = (
        (block_experts[:, :, None] == jnp.arange(experts, dtype=jnp.int32)) & block_live[:, :, None]
    ).astype(jnp.int32)
    before = jnp.cumsum(onehot, axis=1) - onehot
    position = jnp.sum(before * onehot, axis=2)
    slot_total = experts * groups * capacity
    offsets = jnp.arange(groups, dtype=jnp.int32)[:, None] * capacity
    target = jnp.where(
        block_live, block_experts * (groups * capacity) + offsets + position, slot_total
    ).reshape(rows_all, top_count)
    slot_hit = target[:, :, None] == jnp.arange(slot_total, dtype=jnp.int32)[None, None, :]
    own_total = experts * capacity
    own_target = jnp.where(
        block_live[0], block_experts[0] * capacity + position[0], own_total
    ).reshape(row_count, top_count)
    own_hit = own_target[:, :, None] == jnp.arange(own_total, dtype=jnp.int32)[None, None, :]
    fill = jnp.any(own_hit, axis=1).astype(jnp.bfloat16).reshape(row_count, experts, capacity)
    outgoing = lax.dot_general(
        fill, column[:row_count], (((0,), (0,)), ((), ())), preferred_element_type=jnp.float32
    ).astype(jnp.bfloat16)
    slot_own = lax.all_to_all(outgoing, "expert", split_axis=0, concat_axis=0, tiled=True)
    slot_other = swap_pair(slot_own)
    by_width = (((2,), (1,)), ((), ()))
    hidden_own = (
        jax.nn.silu(lax.dot_general(slot_own, gate_local, by_width, preferred_element_type=jnp.float32))
        * lax.dot_general(slot_own, up_local, by_width, preferred_element_type=jnp.float32)
    ).astype(jnp.bfloat16)
    hidden_own_peer = swap_pair(hidden_own)
    hidden_other = (
        jax.nn.silu(lax.dot_general(slot_other, gate_local, by_width, preferred_element_type=jnp.float32))
        * lax.dot_general(slot_other, up_local, by_width, preferred_element_type=jnp.float32)
    ).astype(jnp.bfloat16)
    hidden_other_peer = swap_pair(hidden_other)
    shared_gate_value = by_rows(column, shared_gate)
    shared_up_value = by_rows(column, shared_up)
    shared_hidden = (jax.nn.silu(shared_gate_value) * shared_up_value).astype(jnp.bfloat16)
    shared_peer = halves_swapped(swap_pair(shared_hidden))

    unit_count = hidden_own.shape[2]
    down_blocks = down_local.reshape(groups, unit_count, column_width)
    shared_blocks = shared_down.reshape(groups, unit_count, column_width)
    down_mine = lax.dynamic_index_in_dim(down_blocks, me, 0, keepdims=False)
    down_peer = lax.dynamic_index_in_dim(down_blocks, 1 - me, 0, keepdims=False)
    shared_mine = lax.dynamic_index_in_dim(shared_blocks, me, 0, keepdims=False)
    shared_other = lax.dynamic_index_in_dim(shared_blocks, 1 - me, 0, keepdims=False)
    by_units = (((2,), (0,)), ((), ()))
    out_own = lax.dot_general(
        hidden_own, down_mine, by_units, preferred_element_type=jnp.float32
    ) + lax.dot_general(hidden_other_peer, down_peer, by_units, preferred_element_type=jnp.float32)
    out_other = lax.dot_general(
        hidden_other, down_mine, by_units, preferred_element_type=jnp.float32
    ) + lax.dot_general(hidden_own_peer, down_peer, by_units, preferred_element_type=jnp.float32)
    shared = jnp.dot(shared_hidden, shared_mine, preferred_element_type=jnp.float32) + jnp.dot(
        shared_peer, shared_other, preferred_element_type=jnp.float32
    )
    expert_out = jnp.stack([out_own.astype(jnp.bfloat16), out_other.astype(jnp.bfloat16)], axis=1)
    returned = lax.all_to_all(expert_out, "expert", split_axis=0, concat_axis=0, tiled=True)
    combine = jnp.sum(
        jnp.where(slot_hit, weights[:, :, None], jnp.zeros((), jnp.bfloat16)), axis=1
    ).astype(jnp.bfloat16)
    combine = combine.reshape(rows_all, experts, groups, capacity)
    routed = lax.dot_general(
        combine, returned, (((1, 2, 3), (0, 1, 2)), ((), ())), preferred_element_type=jnp.float32
    )
    combined = jnp.where(row_live[:, None], routed + shared, 0.0)
    summed = in_axis_order(first, combined[:row_count], swap_pair(combined[row_count:]), 1)
    stream_sum = stream_in + summed
    stream = stream_sum.astype(jnp.bfloat16)[None, None]
    normed = rms_scale(stream_sum, gain_out).astype(jnp.bfloat16)[None, None]
    return (stream, normed)


def shards(*args):
    if lax.axis_size("dp") == 2:
        return shards_pair(*args)
    return shards_general(*args)


def solution(mesh):
    placed = (
        P("expert", "dp", None, None),
        P("expert", "dp", None, None),
        P(None, "dp"),
        P(),
        P(None, "dp"),
        P("expert", None, None, None),
        P(None, "expert"),
        P("expert", "dp", None),
        P("expert", "dp", None),
        P("expert", None, "dp"),
        P("dp", None),
        P("dp", None),
        P(None, "dp"),
        P(),
    )
    return jax.shard_map(
        shards,
        mesh=mesh,
        in_specs=placed,
        out_specs=(P("expert", "dp", None, None), P("expert", "dp", None, None)),
        check_vma=False,
    )
```

```python
import jax
import jax.numpy as jnp
from jax import lax
from jax.sharding import PartitionSpec as P


def rms_scale(features, scale_gain):
    return (
        features
        * lax.rsqrt(jnp.mean(features * features, axis=-1, keepdims=True) + 1e-06)
        * scale_gain
    )


def by_rows(left, weight_rows):
    return lax.dot_general(
        left, weight_rows, (((1,), (1,)), ((), ())), preferred_element_type=jnp.float32
    )


def fill_slots(features, targets, slot_total, top_count):
    entries = jnp.arange(targets.shape[0], dtype=jnp.int32)
    source = jnp.full((slot_total,), -1, jnp.int32).at[targets].set(entries, mode="drop")
    chosen = jnp.take(features, jnp.maximum(source, 0) // top_count, axis=0)
    return jnp.where((source >= 0)[:, None], chosen, jnp.zeros_like(chosen))


def shards_general(
    attention,
    residual,
    out_proj,
    gain_in,
    router,
    expert_ids,
    live_rows,
    expert_gate,
    expert_up,
    expert_down,
    shared_gate,
    shared_up,
    shared_down,
    gain_out,
):
    groups = lax.axis_size("dp")
    experts = lax.axis_size("expert")
    row_count = attention.shape[2]
    feature_width = residual.shape[3]
    top_count = expert_ids.shape[3]
    capacity = max(2, (2 * row_count * top_count + experts - 1) // experts)
    gate_local = expert_gate[0]
    up_local = expert_up[0]
    down_local = expert_down[0]
    column_width = down_local.shape[1]
    pieces = lax.all_gather(attention, "dp", axis=1, tiled=True)
    flattened = pieces.reshape(-1, pieces.shape[-1])
    product = jnp.dot(flattened, out_proj, preferred_element_type=jnp.float32).astype(jnp.bfloat16)
    columns = product.reshape(pieces.shape[:-1] + (out_proj.shape[1],))
    projected = lax.all_to_all(columns, "dp", split_axis=1, concat_axis=3, tiled=True)[0, 0]
    stream_in = residual[0, 0].astype(jnp.float32) + projected.astype(jnp.float32)
    normal_rows = rms_scale(stream_in, gain_in).astype(jnp.bfloat16)
    column = lax.all_gather(normal_rows[None], "dp", axis=0, tiled=True).reshape(
        groups * row_count, feature_width
    )
    logit_part = jnp.dot(column, router, preferred_element_type=jnp.float32)
    logits = lax.all_gather(logit_part, "dp", axis=1, tiled=True)
    flat_experts = expert_ids[0].reshape(groups * row_count, top_count)
    picked = jnp.take_along_axis(logits, flat_experts, axis=1)
    probabilities = jax.nn.softmax(picked, axis=1)
    row_live = (jnp.arange(row_count, dtype=jnp.int32)[None, :] < live_rows[:, 0][:, None]).reshape(
        groups * row_count
    )
    slot_live = jnp.broadcast_to(row_live[:, None], (groups * row_count, top_count))
    weights = probabilities.astype(jnp.bfloat16) * slot_live.astype(jnp.bfloat16)
    block_experts = flat_experts.reshape(groups, row_count * top_count)
    block_live = slot_live.reshape(groups, row_count * top_count)
    onehot = (
        (block_experts[:, :, None] == jnp.arange(experts, dtype=jnp.int32)) & block_live[:, :, None]
    ).astype(jnp.int32)
    before = jnp.cumsum(onehot, axis=1) - onehot
    position = jnp.sum(before * onehot, axis=2)
    slot_total = experts * groups * capacity
    offsets = jnp.arange(groups, dtype=jnp.int32)[:, None] * capacity
    target = jnp.where(
        block_live, block_experts * (groups * capacity) + offsets + position, slot_total
    ).reshape(-1)
    outgoing = fill_slots(column, target, slot_total, top_count).reshape(
        experts, groups * capacity, feature_width
    )
    slot_rows = lax.all_to_all(outgoing, "expert", split_axis=0, concat_axis=0, tiled=True)
    flattened = slot_rows.reshape(-1, slot_rows.shape[-1])
    gate_value = by_rows(flattened, gate_local)
    up_value = by_rows(flattened, up_local)
    hidden = (jax.nn.silu(gate_value) * up_value).astype(jnp.bfloat16)
    routed_hidden = hidden.reshape(slot_rows.shape[:-1] + (gate_local.shape[0],))
    shared_gate_value = by_rows(column, shared_gate)
    shared_up_value = by_rows(column, shared_up)
    shared_hidden = (jax.nn.silu(shared_gate_value) * shared_up_value).astype(jnp.bfloat16)[None]
    routed_piece = lax.all_gather(routed_hidden, "dp", axis=2, tiled=True)
    shared_piece = lax.all_gather(shared_hidden, "dp", axis=2, tiled=True)
    count = routed_piece.shape[2]
    routed_total = jnp.dot(
        routed_piece.reshape(-1, count), down_local, preferred_element_type=jnp.float32
    )
    shared_total = jnp.dot(
        shared_piece.reshape(-1, shared_piece.shape[2]),
        shared_down,
        preferred_element_type=jnp.float32,
    )
    routed_total, shared = (routed_total, shared_total)
    expert_out = routed_total.astype(jnp.bfloat16).reshape(experts, groups * capacity, column_width)
    returned = lax.all_to_all(
        expert_out, "expert", split_axis=0, concat_axis=0, tiled=True
    ).reshape(slot_total, column_width)
    gathered = jnp.take(returned, jnp.minimum(target, slot_total - 1), axis=0).reshape(
        groups * row_count, top_count, column_width
    )
    routed = jnp.einsum("nk,nkd->nd", weights, gathered, preferred_element_type=jnp.float32)
    combined = jnp.where(row_live[:, None], routed + shared, 0.0).reshape(
        groups, row_count, column_width
    )
    summed = lax.all_to_all(combined, "dp", split_axis=0, concat_axis=2, tiled=True)[0]
    stream_sum = stream_in + summed
    stream = stream_sum.astype(jnp.bfloat16)[None, None]
    normed = rms_scale(stream_sum, gain_out).astype(jnp.bfloat16)[None, None]
    return (stream, normed)


def swap_pair(x):
    return lax.ppermute(x, "dp", [(0, 1), (1, 0)])


def halves_swapped(x):
    half = x.shape[0] // 2
    return jnp.concatenate([x[half:], x[:half]], axis=0)


def in_axis_order(first, mine, peer, axis):
    return jnp.where(
        first, jnp.concatenate([mine, peer], axis=axis), jnp.concatenate([peer, mine], axis=axis)
    )


def shards_pair(
    attention,
    residual,
    out_proj,
    gain_in,
    router,
    expert_ids,
    live_rows,
    expert_gate,
    expert_up,
    expert_down,
    shared_gate,
    shared_up,
    shared_down,
    gain_out,
):
    groups = 2
    experts = lax.axis_size("expert")
    me = lax.axis_index("dp")
    first = me == 0
    row_count = attention.shape[2]
    top_count = expert_ids.shape[3]
    capacity = max(2, (2 * row_count * top_count + experts - 1) // experts)
    gate_local = expert_gate[0]
    up_local = expert_up[0]
    down_local = expert_down[0]
    column_width = down_local.shape[1]
    rows_all = groups * row_count

    attention_mine = attention[0, 0]
    residual_mine = residual[0, 0]
    pieces = jnp.concatenate([attention_mine, swap_pair(attention_mine)], axis=0)
    residual_all = jnp.concatenate([residual_mine, swap_pair(residual_mine)], axis=0)
    product = jnp.dot(pieces, out_proj, preferred_element_type=jnp.float32).astype(jnp.bfloat16)
    projected = in_axis_order(first, product, halves_swapped(swap_pair(product)), 1)
    stream_all = residual_all.astype(jnp.float32) + projected.astype(jnp.float32)
    column = rms_scale(stream_all, gain_in).astype(jnp.bfloat16)
    stream_in = stream_all[:row_count]
    logit_part = jnp.dot(column, router, preferred_element_type=jnp.float32)
    logits = in_axis_order(first, logit_part, halves_swapped(swap_pair(logit_part)), 1)

    ids = expert_ids[0]
    ids_local = jnp.where(first, ids, ids[::-1])
    counts = live_rows[:, 0]
    counts_local = jnp.where(first, counts, counts[::-1])
    group_of_block = jnp.where(first, jnp.arange(groups), jnp.arange(groups)[::-1]).astype(jnp.int32)

    flat_experts = ids_local.reshape(rows_all, top_count)
    picked = jnp.take_along_axis(logits, flat_experts, axis=1)
    probabilities = jax.nn.softmax(picked, axis=1)
    row_live = (jnp.arange(row_count, dtype=jnp.int32)[None, :] < counts_local[:, None]).reshape(
        rows_all
    )
    slot_live = jnp.broadcast_to(row_live[:, None], (rows_all, top_count))
    weights = probabilities.astype(jnp.bfloat16) * slot_live.astype(jnp.bfloat16)
    block_experts = flat_experts.reshape(groups, row_count * top_count)
    block_live = slot_live.reshape(groups, row_count * top_count)
    onehot = (
        (block_experts[:, :, None] == jnp.arange(experts, dtype=jnp.int32)) & block_live[:, :, None]
    ).astype(jnp.int32)
    before = jnp.cumsum(onehot, axis=1) - onehot
    position = jnp.sum(before * onehot, axis=2)
    slot_total = experts * groups * capacity
    offsets = group_of_block[:, None] * capacity
    target = jnp.where(
        block_live, block_experts * (groups * capacity) + offsets + position, slot_total
    ).reshape(rows_all, top_count)
    slot_hit = target[:, :, None] == jnp.arange(slot_total, dtype=jnp.int32)[None, None, :]
    fill = jnp.any(slot_hit, axis=1).astype(jnp.bfloat16)
    outgoing = lax.dot_general(
        fill, column, (((0,), (0,)), ((), ())), preferred_element_type=jnp.float32
    ).astype(jnp.bfloat16).reshape(experts, groups * capacity, column.shape[1])
    slot_rows = lax.all_to_all(outgoing, "expert", split_axis=0, concat_axis=0, tiled=True)
    flattened = slot_rows.reshape(-1, slot_rows.shape[-1])
    unit_total = gate_local.shape[0]
    both = by_rows(flattened, jnp.concatenate([gate_local, up_local], axis=0))
    hidden = (jax.nn.silu(both[:, :unit_total]) * both[:, unit_total:]).astype(jnp.bfloat16)
    hidden_peer = swap_pair(hidden)
    shared_gate_value = by_rows(column, shared_gate)
    shared_up_value = by_rows(column, shared_up)
    shared_hidden = (jax.nn.silu(shared_gate_value) * shared_up_value).astype(jnp.bfloat16)
    shared_peer = halves_swapped(swap_pair(shared_hidden))

    unit_count = hidden.shape[1]
    down_blocks = down_local.reshape(groups, unit_count, column_width)
    shared_blocks = shared_down.reshape(groups, unit_count, column_width)
    down_mine = lax.dynamic_index_in_dim(down_blocks, me, 0, keepdims=False)
    down_peer = lax.dynamic_index_in_dim(down_blocks, 1 - me, 0, keepdims=False)
    shared_mine = lax.dynamic_index_in_dim(shared_blocks, me, 0, keepdims=False)
    shared_other = lax.dynamic_index_in_dim(shared_blocks, 1 - me, 0, keepdims=False)
    routed_total = jnp.dot(hidden, down_mine, preferred_element_type=jnp.float32) + jnp.dot(
        hidden_peer, down_peer, preferred_element_type=jnp.float32
    )
    shared = jnp.dot(shared_hidden, shared_mine, preferred_element_type=jnp.float32) + jnp.dot(
        shared_peer, shared_other, preferred_element_type=jnp.float32
    )
    expert_out = routed_total.astype(jnp.bfloat16).reshape(experts, groups * capacity, column_width)
    returned = lax.all_to_all(
        expert_out, "expert", split_axis=0, concat_axis=0, tiled=True
    ).reshape(slot_total, column_width)
    combine = jnp.sum(
        jnp.where(slot_hit, weights[:, :, None], jnp.zeros((), jnp.bfloat16)), axis=1
    ).astype(jnp.bfloat16)
    routed = jnp.dot(combine, returned, preferred_element_type=jnp.float32)
    combined = jnp.where(row_live[:, None], routed + shared, 0.0)
    summed = in_axis_order(first, combined[:row_count], swap_pair(combined[row_count:]), 1)
    stream_sum = stream_in + summed
    stream = stream_sum.astype(jnp.bfloat16)[None, None]
    normed = rms_scale(stream_sum, gain_out).astype(jnp.bfloat16)[None, None]
    return (stream, normed)


def shards(*args):
    if lax.axis_size("dp") == 2:
        return shards_pair(*args)
    return shards_general(*args)


def solution(mesh):
    placed = (
        P("expert", "dp", None, None),
        P("expert", "dp", None, None),
        P(None, "dp"),
        P(),
        P(None, "dp"),
        P("expert", None, None, None),
        P(None, "expert"),
        P("expert", "dp", None),
        P("expert", "dp", None),
        P("expert", None, "dp"),
        P("dp", None),
        P("dp", None),
        P(None, "dp"),
        P(),
    )
    return jax.shard_map(
        shards,
        mesh=mesh,
        in_specs=placed,
        out_specs=(P("expert", "dp", None, None), P("expert", "dp", None, None)),
        check_vma=False,
    )
```

```python
import jax
import jax.numpy as jnp
from jax import lax
from jax.sharding import PartitionSpec as P


def rms_scale(features, scale_gain):
    return (
        features
        * lax.rsqrt(jnp.mean(features * features, axis=-1, keepdims=True) + 1e-06)
        * scale_gain
    )


def by_rows(left, weight_rows):
    return lax.dot_general(
        left, weight_rows, (((1,), (1,)), ((), ())), preferred_element_type=jnp.float32
    )


def fill_slots(features, targets, slot_total, top_count):
    entries = jnp.arange(targets.shape[0], dtype=jnp.int32)
    source = jnp.full((slot_total,), -1, jnp.int32).at[targets].set(entries, mode="drop")
    chosen = jnp.take(features, jnp.maximum(source, 0) // top_count, axis=0)
    return jnp.where((source >= 0)[:, None], chosen, jnp.zeros_like(chosen))


def shards_general(
    attention,
    residual,
    out_proj,
    gain_in,
    router,
    expert_ids,
    live_rows,
    expert_gate,
    expert_up,
    expert_down,
    shared_gate,
    shared_up,
    shared_down,
    gain_out,
):
    groups = lax.axis_size("dp")
    experts = lax.axis_size("expert")
    row_count = attention.shape[2]
    feature_width = residual.shape[3]
    top_count = expert_ids.shape[3]
    capacity = max(2, (2 * row_count * top_count + experts - 1) // experts)
    gate_local = expert_gate[0]
    up_local = expert_up[0]
    down_local = expert_down[0]
    column_width = down_local.shape[1]
    pieces = lax.all_gather(attention, "dp", axis=1, tiled=True)
    flattened = pieces.reshape(-1, pieces.shape[-1])
    product = jnp.dot(flattened, out_proj, preferred_element_type=jnp.float32).astype(jnp.bfloat16)
    columns = product.reshape(pieces.shape[:-1] + (out_proj.shape[1],))
    projected = lax.all_to_all(columns, "dp", split_axis=1, concat_axis=3, tiled=True)[0, 0]
    stream_in = residual[0, 0].astype(jnp.float32) + projected.astype(jnp.float32)
    normal_rows = rms_scale(stream_in, gain_in).astype(jnp.bfloat16)
    column = lax.all_gather(normal_rows[None], "dp", axis=0, tiled=True).reshape(
        groups * row_count, feature_width
    )
    logit_part = jnp.dot(column, router, preferred_element_type=jnp.float32)
    logits = lax.all_gather(logit_part, "dp", axis=1, tiled=True)
    flat_experts = expert_ids[0].reshape(groups * row_count, top_count)
    picked = jnp.take_along_axis(logits, flat_experts, axis=1)
    probabilities = jax.nn.softmax(picked, axis=1)
    row_live = (jnp.arange(row_count, dtype=jnp.int32)[None, :] < live_rows[:, 0][:, None]).reshape(
        groups * row_count
    )
    slot_live = jnp.broadcast_to(row_live[:, None], (groups * row_count, top_count))
    weights = probabilities.astype(jnp.bfloat16) * slot_live.astype(jnp.bfloat16)
    block_experts = flat_experts.reshape(groups, row_count * top_count)
    block_live = slot_live.reshape(groups, row_count * top_count)
    onehot = (
        (block_experts[:, :, None] == jnp.arange(experts, dtype=jnp.int32)) & block_live[:, :, None]
    ).astype(jnp.int32)
    before = jnp.cumsum(onehot, axis=1) - onehot
    position = jnp.sum(before * onehot, axis=2)
    slot_total = experts * groups * capacity
    offsets = jnp.arange(groups, dtype=jnp.int32)[:, None] * capacity
    target = jnp.where(
        block_live, block_experts * (groups * capacity) + offsets + position, slot_total
    ).reshape(-1)
    outgoing = fill_slots(column, target, slot_total, top_count).reshape(
        experts, groups * capacity, feature_width
    )
    slot_rows = lax.all_to_all(outgoing, "expert", split_axis=0, concat_axis=0, tiled=True)
    flattened = slot_rows.reshape(-1, slot_rows.shape[-1])
    gate_value = by_rows(flattened, gate_local)
    up_value = by_rows(flattened, up_local)
    hidden = (jax.nn.silu(gate_value) * up_value).astype(jnp.bfloat16)
    routed_hidden = hidden.reshape(slot_rows.shape[:-1] + (gate_local.shape[0],))
    shared_gate_value = by_rows(column, shared_gate)
    shared_up_value = by_rows(column, shared_up)
    shared_hidden = (jax.nn.silu(shared_gate_value) * shared_up_value).astype(jnp.bfloat16)[None]
    routed_piece = lax.all_gather(routed_hidden, "dp", axis=2, tiled=True)
    shared_piece = lax.all_gather(shared_hidden, "dp", axis=2, tiled=True)
    count = routed_piece.shape[2]
    routed_total = jnp.dot(
        routed_piece.reshape(-1, count), down_local, preferred_element_type=jnp.float32
    )
    shared_total = jnp.dot(
        shared_piece.reshape(-1, shared_piece.shape[2]),
        shared_down,
        preferred_element_type=jnp.float32,
    )
    routed_total, shared = (routed_total, shared_total)
    expert_out = routed_total.astype(jnp.bfloat16).reshape(experts, groups * capacity, column_width)
    returned = lax.all_to_all(
        expert_out, "expert", split_axis=0, concat_axis=0, tiled=True
    ).reshape(slot_total, column_width)
    gathered = jnp.take(returned, jnp.minimum(target, slot_total - 1), axis=0).reshape(
        groups * row_count, top_count, column_width
    )
    routed = jnp.einsum("nk,nkd->nd", weights, gathered, preferred_element_type=jnp.float32)
    combined = jnp.where(row_live[:, None], routed + shared, 0.0).reshape(
        groups, row_count, column_width
    )
    summed = lax.all_to_all(combined, "dp", split_axis=0, concat_axis=2, tiled=True)[0]
    stream_sum = stream_in + summed
    stream = stream_sum.astype(jnp.bfloat16)[None, None]
    normed = rms_scale(stream_sum, gain_out).astype(jnp.bfloat16)[None, None]
    return (stream, normed)


def swap_pair(x):
    return lax.ppermute(x, "dp", [(0, 1), (1, 0)])


def halves_swapped(x):
    half = x.shape[0] // 2
    return jnp.concatenate([x[half:], x[:half]], axis=0)


def in_axis_order(first, mine, peer, axis):
    return jnp.where(
        first, jnp.concatenate([mine, peer], axis=axis), jnp.concatenate([peer, mine], axis=axis)
    )


def shards_pair(
    attention,
    residual,
    out_proj,
    gain_in,
    router,
    expert_ids,
    live_rows,
    expert_gate,
    expert_up,
    expert_down,
    shared_gate,
    shared_up,
    shared_down,
    gain_out,
):
    groups = 2
    experts = lax.axis_size("expert")
    me = lax.axis_index("dp")
    first = me == 0
    row_count = attention.shape[2]
    top_count = expert_ids.shape[3]
    capacity = max(2, (2 * row_count * top_count + experts - 1) // experts)
    gate_local = expert_gate[0]
    up_local = expert_up[0]
    down_local = expert_down[0]
    column_width = down_local.shape[1]
    rows_all = groups * row_count

    attention_mine = attention[0, 0]
    residual_mine = residual[0, 0]
    pieces = jnp.concatenate([attention_mine, swap_pair(attention_mine)], axis=0)
    residual_all = jnp.concatenate([residual_mine, swap_pair(residual_mine)], axis=0)
    product = jnp.dot(pieces, out_proj, preferred_element_type=jnp.float32).astype(jnp.bfloat16)
    projected = in_axis_order(first, product, halves_swapped(swap_pair(product)), 1)
    stream_all = residual_all.astype(jnp.float32) + projected.astype(jnp.float32)
    column = rms_scale(stream_all, gain_in).astype(jnp.bfloat16)
    stream_in = stream_all[:row_count]
    logit_part = jnp.dot(column, router, preferred_element_type=jnp.float32)
    logits = in_axis_order(first, logit_part, halves_swapped(swap_pair(logit_part)), 1)

    ids = expert_ids[0]
    ids_local = jnp.where(first, ids, ids[::-1])
    counts = live_rows[:, 0]
    counts_local = jnp.where(first, counts, counts[::-1])
    group_of_block = jnp.where(first, jnp.arange(groups), jnp.arange(groups)[::-1]).astype(jnp.int32)

    flat_experts = ids_local.reshape(rows_all, top_count)
    picked = jnp.take_along_axis(logits, flat_experts, axis=1)
    probabilities = jax.nn.softmax(picked, axis=1)
    row_live = (jnp.arange(row_count, dtype=jnp.int32)[None, :] < counts_local[:, None]).reshape(
        rows_all
    )
    slot_live = jnp.broadcast_to(row_live[:, None], (rows_all, top_count))
    weights = probabilities.astype(jnp.bfloat16) * slot_live.astype(jnp.bfloat16)
    block_experts = flat_experts.reshape(groups, row_count * top_count)
    block_live = slot_live.reshape(groups, row_count * top_count)
    onehot = (
        (block_experts[:, :, None] == jnp.arange(experts, dtype=jnp.int32)) & block_live[:, :, None]
    ).astype(jnp.int32)
    before = jnp.cumsum(onehot, axis=1) - onehot
    position = jnp.sum(before * onehot, axis=2)
    slot_total = experts * groups * capacity
    offsets = group_of_block[:, None] * capacity
    target = jnp.where(
        block_live, block_experts * (groups * capacity) + offsets + position, slot_total
    ).reshape(rows_all, top_count)
    slot_hit = target[:, :, None] == jnp.arange(slot_total, dtype=jnp.int32)[None, None, :]
    fill = jnp.any(slot_hit, axis=1).astype(jnp.bfloat16)
    outgoing = lax.dot_general(
        fill, column, (((0,), (0,)), ((), ())), preferred_element_type=jnp.float32
    ).astype(jnp.bfloat16).reshape(experts, groups * capacity, column.shape[1])
    slot_rows = lax.all_to_all(outgoing, "expert", split_axis=0, concat_axis=0, tiled=True)
    flattened = slot_rows.reshape(-1, slot_rows.shape[-1])
    unit_total = gate_local.shape[0]
    both = lax.dot_general(
        jnp.concatenate([gate_local, up_local], axis=0),
        flattened,
        (((1,), (1,)), ((), ())),
        preferred_element_type=jnp.float32,
    )
    hidden_t = (jax.nn.silu(both[:unit_total]) * both[unit_total:]).astype(jnp.bfloat16)
    hidden_peer_t = swap_pair(hidden_t)
    shared_gate_value = by_rows(column, shared_gate)
    shared_up_value = by_rows(column, shared_up)
    shared_hidden = (jax.nn.silu(shared_gate_value) * shared_up_value).astype(jnp.bfloat16)
    shared_peer = halves_swapped(swap_pair(shared_hidden))

    unit_count = hidden_t.shape[0]
    down_blocks = down_local.reshape(groups, unit_count, column_width)
    shared_blocks = shared_down.reshape(groups, unit_count, column_width)
    down_mine = lax.dynamic_index_in_dim(down_blocks, me, 0, keepdims=False)
    down_peer = lax.dynamic_index_in_dim(down_blocks, 1 - me, 0, keepdims=False)
    shared_mine = lax.dynamic_index_in_dim(shared_blocks, me, 0, keepdims=False)
    shared_other = lax.dynamic_index_in_dim(shared_blocks, 1 - me, 0, keepdims=False)
    by_units = (((0,), (0,)), ((), ()))
    routed_total = lax.dot_general(
        hidden_t, down_mine, by_units, preferred_element_type=jnp.float32
    ) + lax.dot_general(hidden_peer_t, down_peer, by_units, preferred_element_type=jnp.float32)
    shared = jnp.dot(shared_hidden, shared_mine, preferred_element_type=jnp.float32) + jnp.dot(
        shared_peer, shared_other, preferred_element_type=jnp.float32
    )
    expert_out = routed_total.astype(jnp.bfloat16).reshape(experts, groups * capacity, column_width)
    returned = lax.all_to_all(
        expert_out, "expert", split_axis=0, concat_axis=0, tiled=True
    ).reshape(slot_total, column_width)
    combine = jnp.sum(
        jnp.where(slot_hit, weights[:, :, None], jnp.zeros((), jnp.bfloat16)), axis=1
    ).astype(jnp.bfloat16)
    routed = jnp.dot(combine, returned, preferred_element_type=jnp.float32)
    combined = jnp.where(row_live[:, None], routed + shared, 0.0)
    summed = in_axis_order(first, combined[:row_count], swap_pair(combined[row_count:]), 1)
    stream_sum = stream_in + summed
    stream = stream_sum.astype(jnp.bfloat16)[None, None]
    normed = rms_scale(stream_sum, gain_out).astype(jnp.bfloat16)[None, None]
    return (stream, normed)


def shards(*args):
    if lax.axis_size("dp") == 2:
        return shards_pair(*args)
    return shards_general(*args)


def solution(mesh):
    placed = (
        P("expert", "dp", None, None),
        P("expert", "dp", None, None),
        P(None, "dp"),
        P(),
        P(None, "dp"),
        P("expert", None, None, None),
        P(None, "expert"),
        P("expert", "dp", None),
        P("expert", "dp", None),
        P("expert", None, "dp"),
        P("dp", None),
        P("dp", None),
        P(None, "dp"),
        P(),
    )
    return jax.shard_map(
        shards,
        mesh=mesh,
        in_specs=placed,
        out_specs=(P("expert", "dp", None, None), P("expert", "dp", None, None)),
        check_vma=False,
    )
```

```python
import jax
import jax.numpy as jnp
from jax import lax
from jax.sharding import PartitionSpec as P


def rms_scale(features, scale_gain):
    return (
        features
        * lax.rsqrt(jnp.mean(features * features, axis=-1, keepdims=True) + 1e-06)
        * scale_gain
    )


def by_rows(left, weight_rows):
    return lax.dot_general(
        left, weight_rows, (((1,), (1,)), ((), ())), preferred_element_type=jnp.float32
    )


def fill_slots(features, targets, slot_total, top_count):
    entries = jnp.arange(targets.shape[0], dtype=jnp.int32)
    source = jnp.full((slot_total,), -1, jnp.int32).at[targets].set(entries, mode="drop")
    chosen = jnp.take(features, jnp.maximum(source, 0) // top_count, axis=0)
    return jnp.where((source >= 0)[:, None], chosen, jnp.zeros_like(chosen))


def shards_general(
    attention,
    residual,
    out_proj,
    gain_in,
    router,
    expert_ids,
    live_rows,
    expert_gate,
    expert_up,
    expert_down,
    shared_gate,
    shared_up,
    shared_down,
    gain_out,
):
    groups = lax.axis_size("dp")
    experts = lax.axis_size("expert")
    row_count = attention.shape[2]
    feature_width = residual.shape[3]
    top_count = expert_ids.shape[3]
    capacity = max(2, (2 * row_count * top_count + experts - 1) // experts)
    gate_local = expert_gate[0]
    up_local = expert_up[0]
    down_local = expert_down[0]
    column_width = down_local.shape[1]
    pieces = lax.all_gather(attention, "dp", axis=1, tiled=True)
    flattened = pieces.reshape(-1, pieces.shape[-1])
    product = jnp.dot(flattened, out_proj, preferred_element_type=jnp.float32).astype(jnp.bfloat16)
    columns = product.reshape(pieces.shape[:-1] + (out_proj.shape[1],))
    projected = lax.all_to_all(columns, "dp", split_axis=1, concat_axis=3, tiled=True)[0, 0]
    stream_in = residual[0, 0].astype(jnp.float32) + projected.astype(jnp.float32)
    normal_rows = rms_scale(stream_in, gain_in).astype(jnp.bfloat16)
    column = lax.all_gather(normal_rows[None], "dp", axis=0, tiled=True).reshape(
        groups * row_count, feature_width
    )
    logit_part = jnp.dot(column, router, preferred_element_type=jnp.float32)
    logits = lax.all_gather(logit_part, "dp", axis=1, tiled=True)
    flat_experts = expert_ids[0].reshape(groups * row_count, top_count)
    picked = jnp.take_along_axis(logits, flat_experts, axis=1)
    probabilities = jax.nn.softmax(picked, axis=1)
    row_live = (jnp.arange(row_count, dtype=jnp.int32)[None, :] < live_rows[:, 0][:, None]).reshape(
        groups * row_count
    )
    slot_live = jnp.broadcast_to(row_live[:, None], (groups * row_count, top_count))
    weights = probabilities.astype(jnp.bfloat16) * slot_live.astype(jnp.bfloat16)
    block_experts = flat_experts.reshape(groups, row_count * top_count)
    block_live = slot_live.reshape(groups, row_count * top_count)
    onehot = (
        (block_experts[:, :, None] == jnp.arange(experts, dtype=jnp.int32)) & block_live[:, :, None]
    ).astype(jnp.int32)
    before = jnp.cumsum(onehot, axis=1) - onehot
    position = jnp.sum(before * onehot, axis=2)
    slot_total = experts * groups * capacity
    offsets = jnp.arange(groups, dtype=jnp.int32)[:, None] * capacity
    target = jnp.where(
        block_live, block_experts * (groups * capacity) + offsets + position, slot_total
    ).reshape(-1)
    outgoing = fill_slots(column, target, slot_total, top_count).reshape(
        experts, groups * capacity, feature_width
    )
    slot_rows = lax.all_to_all(outgoing, "expert", split_axis=0, concat_axis=0, tiled=True)
    flattened = slot_rows.reshape(-1, slot_rows.shape[-1])
    gate_value = by_rows(flattened, gate_local)
    up_value = by_rows(flattened, up_local)
    hidden = (jax.nn.silu(gate_value) * up_value).astype(jnp.bfloat16)
    routed_hidden = hidden.reshape(slot_rows.shape[:-1] + (gate_local.shape[0],))
    shared_gate_value = by_rows(column, shared_gate)
    shared_up_value = by_rows(column, shared_up)
    shared_hidden = (jax.nn.silu(shared_gate_value) * shared_up_value).astype(jnp.bfloat16)[None]
    routed_piece = lax.all_gather(routed_hidden, "dp", axis=2, tiled=True)
    shared_piece = lax.all_gather(shared_hidden, "dp", axis=2, tiled=True)
    count = routed_piece.shape[2]
    routed_total = jnp.dot(
        routed_piece.reshape(-1, count), down_local, preferred_element_type=jnp.float32
    )
    shared_total = jnp.dot(
        shared_piece.reshape(-1, shared_piece.shape[2]),
        shared_down,
        preferred_element_type=jnp.float32,
    )
    routed_total, shared = (routed_total, shared_total)
    expert_out = routed_total.astype(jnp.bfloat16).reshape(experts, groups * capacity, column_width)
    returned = lax.all_to_all(
        expert_out, "expert", split_axis=0, concat_axis=0, tiled=True
    ).reshape(slot_total, column_width)
    gathered = jnp.take(returned, jnp.minimum(target, slot_total - 1), axis=0).reshape(
        groups * row_count, top_count, column_width
    )
    routed = jnp.einsum("nk,nkd->nd", weights, gathered, preferred_element_type=jnp.float32)
    combined = jnp.where(row_live[:, None], routed + shared, 0.0).reshape(
        groups, row_count, column_width
    )
    summed = lax.all_to_all(combined, "dp", split_axis=0, concat_axis=2, tiled=True)[0]
    stream_sum = stream_in + summed
    stream = stream_sum.astype(jnp.bfloat16)[None, None]
    normed = rms_scale(stream_sum, gain_out).astype(jnp.bfloat16)[None, None]
    return (stream, normed)


def swap_pair(x):
    return lax.ppermute(x, "dp", [(0, 1), (1, 0)])


def halves_swapped(x):
    half = x.shape[0] // 2
    return jnp.concatenate([x[half:], x[:half]], axis=0)


def in_axis_order(first, mine, peer, axis):
    return jnp.where(
        first, jnp.concatenate([mine, peer], axis=axis), jnp.concatenate([peer, mine], axis=axis)
    )


def shards_pair(
    attention,
    residual,
    out_proj,
    gain_in,
    router,
    expert_ids,
    live_rows,
    expert_gate,
    expert_up,
    expert_down,
    shared_gate,
    shared_up,
    shared_down,
    gain_out,
):
    groups = 2
    experts = lax.axis_size("expert")
    me = lax.axis_index("dp")
    first = me == 0
    row_count = attention.shape[2]
    top_count = expert_ids.shape[3]
    capacity = max(2, (2 * row_count * top_count + experts - 1) // experts)
    gate_local = expert_gate[0]
    up_local = expert_up[0]
    down_local = expert_down[0]
    column_width = down_local.shape[1]
    rows_all = groups * row_count

    attention_mine = attention[0, 0]
    residual_mine = residual[0, 0]
    pieces = jnp.concatenate([attention_mine, swap_pair(attention_mine)], axis=0)
    residual_all = jnp.concatenate([residual_mine, swap_pair(residual_mine)], axis=0)
    product = jnp.dot(pieces, out_proj, preferred_element_type=jnp.float32).astype(jnp.bfloat16)
    projected = in_axis_order(first, product, halves_swapped(swap_pair(product)), 1)
    stream_all = residual_all.astype(jnp.float32) + projected.astype(jnp.float32)
    column = rms_scale(stream_all, gain_in).astype(jnp.bfloat16)
    stream_in = stream_all[:row_count]
    logit_part = jnp.dot(column, router, preferred_element_type=jnp.float32)
    logits = in_axis_order(first, logit_part, halves_swapped(swap_pair(logit_part)), 1)

    ids = expert_ids[0]
    ids_local = jnp.where(first, ids, ids[::-1])
    counts = live_rows[:, 0]
    counts_local = jnp.where(first, counts, counts[::-1])
    group_of_block = jnp.where(first, jnp.arange(groups), jnp.arange(groups)[::-1]).astype(jnp.int32)

    flat_experts = ids_local.reshape(rows_all, top_count)
    picked = jnp.take_along_axis(logits, flat_experts, axis=1)
    probabilities = jax.nn.softmax(picked, axis=1)
    row_live = (jnp.arange(row_count, dtype=jnp.int32)[None, :] < counts_local[:, None]).reshape(
        rows_all
    )
    slot_live = jnp.broadcast_to(row_live[:, None], (rows_all, top_count))
    weights = probabilities.astype(jnp.bfloat16) * slot_live.astype(jnp.bfloat16)
    block_experts = flat_experts.reshape(groups, row_count * top_count)
    block_live = slot_live.reshape(groups, row_count * top_count)
    onehot = (
        (block_experts[:, :, None] == jnp.arange(experts, dtype=jnp.int32)) & block_live[:, :, None]
    ).astype(jnp.int32)
    before = jnp.cumsum(onehot, axis=1) - onehot
    position = jnp.sum(before * onehot, axis=2)
    slot_total = experts * groups * capacity
    offsets = group_of_block[:, None] * capacity
    target = jnp.where(
        block_live, block_experts * (groups * capacity) + offsets + position, slot_total
    ).reshape(rows_all, top_count)
    slot_hit = target[:, :, None] == jnp.arange(slot_total, dtype=jnp.int32)[None, None, :]
    fill = jnp.any(slot_hit, axis=1).astype(jnp.bfloat16)
    outgoing = lax.dot_general(
        fill, column, (((0,), (0,)), ((), ())), preferred_element_type=jnp.float32
    ).astype(jnp.bfloat16).reshape(experts, groups * capacity, column.shape[1])
    slot_rows = lax.all_to_all(outgoing, "expert", split_axis=0, concat_axis=0, tiled=True)
    flattened = slot_rows.reshape(-1, slot_rows.shape[-1])
    unit_total = gate_local.shape[0]
    both = lax.dot_general(
        jnp.concatenate([gate_local, up_local], axis=0),
        flattened,
        (((1,), (1,)), ((), ())),
        preferred_element_type=jnp.float32,
    )
    hidden_t = (jax.nn.silu(both[:unit_total]) * both[unit_total:]).astype(jnp.bfloat16)
    hidden_peer_t = swap_pair(hidden_t)
    shared_gate_value = by_rows(column, shared_gate)
    shared_up_value = by_rows(column, shared_up)
    shared_hidden = (jax.nn.silu(shared_gate_value) * shared_up_value).astype(jnp.bfloat16)
    shared_peer = halves_swapped(swap_pair(shared_hidden))

    unit_count = hidden_t.shape[0]
    down_blocks = down_local.reshape(groups, unit_count, column_width)
    shared_blocks = shared_down.reshape(groups, unit_count, column_width)
    down_mine = lax.dynamic_index_in_dim(down_blocks, me, 0, keepdims=False)
    down_peer = lax.dynamic_index_in_dim(down_blocks, 1 - me, 0, keepdims=False)
    shared_mine = lax.dynamic_index_in_dim(shared_blocks, me, 0, keepdims=False)
    shared_other = lax.dynamic_index_in_dim(shared_blocks, 1 - me, 0, keepdims=False)
    by_units = (((0,), (0,)), ((), ()))
    routed_total = lax.dot_general(
        hidden_t, down_mine, by_units, preferred_element_type=jnp.float32
    ) + lax.dot_general(hidden_peer_t, down_peer, by_units, preferred_element_type=jnp.float32)
    shared = jnp.dot(shared_hidden, shared_mine, preferred_element_type=jnp.float32) + jnp.dot(
        shared_peer, shared_other, preferred_element_type=jnp.float32
    )
    expert_out = routed_total.astype(jnp.bfloat16).reshape(experts, groups * capacity, column_width)
    returned = lax.all_to_all(
        expert_out, "expert", split_axis=0, concat_axis=0, tiled=True
    ).reshape(slot_total, column_width)
    combine = jnp.sum(
        jnp.where(slot_hit, weights[:, :, None], jnp.zeros((), jnp.bfloat16)), axis=1
    ).astype(jnp.bfloat16)
    routed_peer = jnp.dot(combine[row_count:], returned, preferred_element_type=jnp.float32)
    combined_peer = jnp.where(row_live[row_count:, None], routed_peer + shared[row_count:], 0.0)
    from_peer = swap_pair(combined_peer)
    routed_mine = jnp.dot(combine[:row_count], returned, preferred_element_type=jnp.float32)
    combined_mine = jnp.where(row_live[:row_count, None], routed_mine + shared[:row_count], 0.0)
    summed = in_axis_order(first, combined_mine, from_peer, 1)
    stream_sum = stream_in + summed
    stream = stream_sum.astype(jnp.bfloat16)[None, None]
    normed = rms_scale(stream_sum, gain_out).astype(jnp.bfloat16)[None, None]
    return (stream, normed)


def shards(*args):
    if lax.axis_size("dp") == 2:
        return shards_pair(*args)
    return shards_general(*args)


def solution(mesh):
    placed = (
        P("expert", "dp", None, None),
        P("expert", "dp", None, None),
        P(None, "dp"),
        P(),
        P(None, "dp"),
        P("expert", None, None, None),
        P(None, "expert"),
        P("expert", "dp", None),
        P("expert", "dp", None),
        P("expert", None, "dp"),
        P("dp", None),
        P("dp", None),
        P(None, "dp"),
        P(),
    )
    return jax.shard_map(
        shards,
        mesh=mesh,
        in_specs=placed,
        out_specs=(P("expert", "dp", None, None), P("expert", "dp", None, None)),
        check_vma=False,
    )
```
